512 devices in a mesh: ctx: 64 (over z, y), head: 8 (over x, core).
Axes of the slice: x: 4, y: 4, z: 16, core: 2. Of those that a mesh axis runs over, the one named last changes fastest.
Arguments:
- queries: bfloat16 [8192, 4096], P(('ctx', 'head')), may hold values from -4.6 to 4.6
- key_states: bfloat16 [8192, 4096], P(('ctx', 'head')), may hold values from -4.6 to 4.6
- value_states: bfloat16 [8192, 4096], P(('ctx', 'head')), may hold values from -6 to 6
- out_grad: bfloat16 [8192, 4096], P(('ctx', 'head')), may hold values from -6 to 6
- random_blocks: int32 [256, 3], replicated, may hold values from 0 to 255, as said below
- global_blocks: int32 [4], replicated, may hold values from 0 to 255, as said below
Outputs:
- query_grad: bfloat16 [8192, 4096], P('ctx', 'head')
- key_grad: bfloat16 [8192, 4096], P('ctx', 'head')
- value_grad: bfloat16 [8192, 4096], P('ctx', 'head')
The draws below stay inside these ranges and needn't reach their ends.
Inputs may be any that keep to these rules, and one draw needn't show every extreme that they name: `random_blocks`: with the blocks i * 4 to i * 4 + 3 called range i: the 12 entries of the rows of range i name blocks of any one range at most 1 times, and some range exactly 1 times. `global_blocks`: 4 different blocks, one of them the last block 255, in any order.
All inputs are finite; a program needn't handle non-finite values.
Results may differ from the reference program's by a relative error of at most 0.0077.
Values may be sent and summed in bfloat16 or wider, within the bound.
No kernel may reach another device: no remote copies, remote signals or barrier semaphores. Data moves between devices by JAX's collectives and lax.ppermute only.
A program may use at most 128 MiB of HBM per device.

```python
import math
import jax
import jax.numpy as jnp
from jax import lax

HEADS = 32
DH = 128
BS = 32
NR = 3
NG = 4
SEQ = 8192
NB = 256
BQ = 4
N_CTX = 64


def base_field(key):
    return jnp.clip(jax.random.normal(key, (SEQ, HEADS * DH), dtype=jnp.float32), -4.6, 4.6)


def draw_queries(key, part):
    values = base_field(jax.random.fold_in(key, 1))
    return values.astype(jnp.bfloat16)


def draw_key_states(key, part):
    values = base_field(jax.random.fold_in(key, 2))
    return values.astype(jnp.bfloat16)


def one_order(subkey):
    return jax.random.permutation(subkey, N_CTX)


def draw_random_blocks(key, part):
    row_width = BQ * NR
    key_list = jax.random.split(jax.random.fold_in(key, 3), N_CTX)
    orders = jax.vmap(one_order)(key_list)
    chosen = jnp.arange(row_width) % N_CTX
    owners = orders[:, chosen]
    offsets = jax.random.randint(jax.random.fold_in(key, 4), (N_CTX, row_width), 0, BQ)
    return (owners * BQ + offsets).astype(jnp.int32).reshape(NB, NR)


def draw_global_blocks(key, part):
    others = jax.random.permutation(jax.random.fold_in(key, 5), NB - 1)[:NG - 1].astype(jnp.int32)
    chosen = jnp.concatenate([jnp.full((1,), NB - 1, jnp.int32), others])
    order = jax.random.permutation(jax.random.fold_in(key, 6), NG)
    return chosen[order].astype(jnp.int32)


def level_of(rng, shape, pieces, smallest, top_value):
    def one(position, shards_of):
        steps = jax.random.uniform(jax.random.fold_in(jax.random.fold_in(rng, 6), position), (shards_of,), jnp.float32, smallest / len(pieces), top_value / len(pieces))
        return jnp.repeat(jnp.exp(steps), shape[position] // shards_of).reshape((-1,) + (1,) * (len(shape) - position - 1))

    level = one(*pieces[0])
    for cut in pieces[1:]:
        level = level * one(*cut)
    return level


def normal_values(key, shape, scale, most, pieces=(), kind=jnp.bfloat16):
    factor_of = level_of(key, shape, pieces, -0.22, 0.18) if pieces else 1.0
    values = jax.random.normal(key, shape, jnp.float32) * scale * factor_of
    return jnp.minimum(jnp.maximum(values, -most), most).astype(kind)


def setup_inputs(seed: int = 0) -> dict:
    arg_keys = jax.random.split(jax.random.key(seed), 7)
    return {
        "queries": draw_queries(jax.random.fold_in(arg_keys[6], 71), 0),
        "key_states": draw_key_states(jax.random.fold_in(arg_keys[6], 71), 0),
        "value_states": normal_values(arg_keys[2], (SEQ, HEADS * DH), 1.0, 6.0, ((0, 512),)),
        "out_grad": normal_values(arg_keys[3], (SEQ, HEADS * DH), 1.0, 6.0, ((0, 512),)),
        "random_blocks": draw_random_blocks(jax.random.fold_in(arg_keys[6], 71), 0),
        "global_blocks": draw_global_blocks(jax.random.fold_in(arg_keys[6], 71), 0),
    }


def settle(partial_value):
    middle = partial_value[:, 3:3 + NR]
    rounded = lax.optimization_barrier(middle.astype(jnp.bfloat16)).astype(jnp.float32)
    return jnp.concatenate([partial_value[:, :3], rounded, partial_value[:, 3 + NR:]], axis=1)

def reference(queries, key_states, value_states, out_grad, random_blocks, global_blocks):
    list_len = 3 + NR + NG
    blocks = jnp.arange(NB, dtype=jnp.int32)
    listed = jnp.concatenate([(blocks - 1)[:, None], blocks[:, None], (blocks + 1)[:, None], random_blocks.astype(jnp.int32), jnp.broadcast_to(global_blocks.astype(jnp.int32)[None, :], (NB, NG))], axis=1)
    usable = (listed >= 0) & (listed < NB)
    clipped = jnp.clip(listed, 0, NB - 1).astype(jnp.int32)
    column_ok = jnp.repeat(usable, BS, axis=1)[:, None, :]
    targets = clipped.reshape(-1)
    inv_root = 1.0 / math.sqrt(DH)

    def one_head(unused, head_index):
        offset = head_index * DH

        def columns_of(array):
            return lax.dynamic_slice_in_dim(array, offset, DH, 1).astype(jnp.float32).reshape(NB, BS, DH)
        query_cols = columns_of(queries)
        key_cols = columns_of(key_states)
        value_cols = columns_of(value_states)
        grad_cols = columns_of(out_grad)
        listed_keys = key_cols[clipped]
        listed_values = value_cols[clipped]
        scores = jnp.einsum('nqd,ngkd->nqgk', query_cols, listed_keys).reshape(NB, BS, list_len * BS) * inv_root
        masked = jnp.where(column_ok, scores, -jnp.inf)
        row_max = lax.optimization_barrier(jnp.max(masked, axis=2, keepdims=True))
        log_total = row_max + jnp.log(lax.optimization_barrier(jnp.sum(jnp.exp(masked - row_max), axis=2, keepdims=True)))
        probs_full = jnp.exp(masked - log_total)
        probs_half = lax.optimization_barrier(probs_full.astype(jnp.bfloat16)).astype(jnp.float32)
        probs_four = probs_half.reshape(NB, BS, list_len, BS)
        outputs = jnp.einsum('nqgk,ngkd->nqd', probs_four, listed_values)
        row_dot = lax.optimization_barrier(jnp.sum(grad_cols * outputs, axis=2, keepdims=True))
        dprobs = jnp.einsum('nqd,ngkd->nqgk', grad_cols, listed_values).reshape(NB, BS, list_len * BS)
        dscores = probs_full * (dprobs - row_dot)
        ds_half = lax.optimization_barrier(dscores.astype(jnp.bfloat16)).astype(jnp.float32)
        ds_four = ds_half.reshape(NB, BS, list_len, BS)
        query_grad = jnp.einsum('nqgk,ngkd->nqd', ds_four, listed_keys) * inv_root
        key_part = jnp.einsum('nqgk,nqd->ngkd', ds_four, query_cols) * inv_root
        value_part = jnp.einsum('nqgk,nqd->ngkd', probs_four, grad_cols)
        key_grad = jnp.zeros((NB, BS, DH), jnp.float32).at[targets].add(settle(key_part).reshape(-1, BS, DH))
        value_grad = jnp.zeros((NB, BS, DH), jnp.float32).at[targets].add(settle(value_part).reshape(-1, BS, DH))
        return (unused, (query_grad.reshape(SEQ, DH).astype(jnp.bfloat16), key_grad.reshape(SEQ, DH).astype(jnp.bfloat16), value_grad.reshape(SEQ, DH).astype(jnp.bfloat16)))
    _, (query_all, key_all, value_all) = lax.scan(one_head, jnp.int32(0), jnp.arange(HEADS, dtype=jnp.int32))

    def arrange(stacked):
        return jnp.transpose(stacked, (1, 0, 2)).reshape(SEQ, HEADS * DH)
    return (arrange(query_all), arrange(key_all), arrange(value_all))
```

```python
import math

import jax
import jax.numpy as jnp
from jax import lax
from jax.sharding import PartitionSpec as P

DH = 128
BS = 32
NR = 3
NG = 4


def with_halo(x, sides, width):
    for axis, dim in sides:
        peers, length = (lax.axis_size(axis), x.shape[dim])
        up = [(i, (i + 1) % peers) for i in range(peers - 1)]
        down = [(j, i) for i, j in up]
        last = lax.slice_in_dim(x, length - width, length, axis=dim)
        first = lax.slice_in_dim(x, 0, width, axis=dim)
        before = lax.ppermute(last, axis, up)
        after = lax.ppermute(first, axis, down)
        x = jnp.concatenate([before, x, after], axis=dim)
    return x


def chunk_sum(x, axis):
    peers = lax.axis_size(axis)
    parts = lax.all_to_all(x.reshape(peers, -1), axis, split_axis=0, concat_axis=0, tiled=True)
    return jnp.sum(parts.astype(jnp.float32), axis=0)


def chunk_share(chunk, axis, shape, dtype):
    peers = lax.axis_size(axis)
    copies = jnp.broadcast_to(chunk.astype(dtype)[None], (peers,) + chunk.shape)
    return lax.all_to_all(copies, axis, split_axis=0, concat_axis=0, tiled=True).reshape(shape)


def all_sum(x, axis):
    return chunk_share(chunk_sum(x, axis), axis, x.shape, x.dtype)


def per_device(queries, key_states, value_states, out_grad, random_blocks, global_blocks):
    groups = lax.axis_size("head")
    rows_in, cols_in = queries.shape
    stacked = jnp.stack([queries, key_states, value_states, out_grad], axis=1)
    stacked = stacked.reshape(rows_in, 4, groups, cols_in // groups)
    stacked = lax.all_to_all(stacked, "head", split_axis=2, concat_axis=0, tiled=True)
    query_rows, key_rows, value_rows, grad_rows = (stacked[:, i, 0] for i in range(4))
    tokens = query_rows.shape[0]
    head_cols = query_rows.shape[1]
    heads_here = head_cols // DH
    blocks_here = tokens // BS
    devices = lax.axis_size("ctx")
    my_index = lax.axis_index("ctx")
    total_blocks = devices * blocks_here
    entries = blocks_here * NR
    capacity = (entries + devices - 1) // devices
    inv_root = 1.0 / math.sqrt(DH)
    kv_rows = jnp.concatenate([key_rows, value_rows], axis=1)
    kv_blocks = kv_rows.reshape(blocks_here, BS, 2 * head_cols)
    extended = with_halo(kv_rows, (("ctx", 0),), BS)
    extended = extended.reshape(blocks_here + 2, BS, 2 * head_cols)
    window = jnp.stack(
        [extended[:blocks_here], extended[1 : blocks_here + 1], extended[2:]], axis=1
    )
    global_owner = global_blocks // blocks_here
    global_offset = global_blocks % blocks_here
    owned = jnp.take(kv_blocks, global_offset, axis=0)
    owned = jnp.where((global_owner == my_index)[:, None, None], owned, jnp.zeros_like(owned))
    global_kv = all_sum(owned, "ctx")
    entry_table = random_blocks.reshape(devices, entries)
    table_owner = entry_table // blocks_here
    table_offset = entry_table % blocks_here
    positions = jnp.arange(entries, dtype=jnp.int32)
    before = positions[None, :] < positions[:, None]
    matches = (table_owner[:, :, None] == table_owner[:, None, :]) & before[None]
    table_slot = jnp.sum(matches.astype(jnp.int32), axis=2)
    my_owner = lax.dynamic_index_in_dim(table_owner, my_index, 0, keepdims=False)
    my_slot = lax.dynamic_index_in_dim(table_slot, my_index, 0, keepdims=False)
    my_target = my_owner * capacity + my_slot
    slot_ids = jnp.arange(capacity, dtype=jnp.int32)
    served = (table_owner == my_index)[:, :, None] & (
        table_slot[:, :, None] == slot_ids[None, None, :]
    )
    served_block = jnp.sum(jnp.where(served, table_offset[:, :, None], 0), axis=1).reshape(-1)
    served_used = jnp.any(served, axis=1).reshape(-1)
    outgoing = jnp.take(kv_blocks, served_block, axis=0)
    incoming = lax.all_to_all(outgoing, "ctx", split_axis=0, concat_axis=0, tiled=True)
    fetched = jnp.take(incoming, my_target, axis=0).reshape(blocks_here, NR, BS, 2 * head_cols)
    near_kv = jnp.concatenate([window, fetched], axis=1)
    near_groups = 3 + NR
    near_count = near_groups * BS
    query_heads = query_rows.reshape(blocks_here, BS, heads_here, DH)
    grad_heads = grad_rows.reshape(blocks_here, BS, heads_here, DH)
    near_keys = near_kv[..., :head_cols].reshape(blocks_here, near_groups, BS, heads_here, DH)
    near_values = near_kv[..., head_cols:].reshape(blocks_here, near_groups, BS, heads_here, DH)
    far_keys = global_kv[..., :head_cols].reshape(NG, BS, heads_here, DH)
    far_values = global_kv[..., head_cols:].reshape(NG, BS, heads_here, DH)
    scores = (
        jnp.concatenate(
            [
                jnp.einsum(
                    "bqhd,bgkhd->bhqgk", query_heads, near_keys, preferred_element_type=jnp.float32
                ).reshape(blocks_here, heads_here, BS, near_count),
                jnp.einsum(
                    "bqhd,gkhd->bhqgk", query_heads, far_keys, preferred_element_type=jnp.float32
                ).reshape(blocks_here, heads_here, BS, NG * BS),
            ],
            axis=3,
        )
        * inv_root
    )
    block_ids = my_index * blocks_here + jnp.arange(blocks_here, dtype=jnp.int32)
    usable = jnp.concatenate(
        [
            (block_ids > 0)[:, None],
            jnp.ones((blocks_here, 1), bool),
            (block_ids < total_blocks - 1)[:, None],
            jnp.ones((blocks_here, NR + NG), bool),
        ],
        axis=1,
    )
    column_ok = jnp.repeat(usable, BS, axis=1)[:, None, None, :]
    masked = jnp.where(column_ok, scores, -jnp.inf)
    row_max = jnp.max(masked, axis=3, keepdims=True)
    log_total = row_max + jnp.log(jnp.sum(jnp.exp(masked - row_max), axis=3, keepdims=True))
    probs_full = jnp.exp(masked - log_total)
    probs_half = probs_full.astype(jnp.bfloat16)
    near_probs = probs_half[..., :near_count].reshape(blocks_here, heads_here, BS, near_groups, BS)
    far_probs = probs_half[..., near_count:].reshape(blocks_here, heads_here, BS, NG, BS)
    outputs = jnp.einsum(
        "bhqgk,bgkhd->bqhd", near_probs, near_values, preferred_element_type=jnp.float32
    ) + jnp.einsum("bhqgk,gkhd->bqhd", far_probs, far_values, preferred_element_type=jnp.float32)
    row_dot = jnp.sum(grad_heads.astype(jnp.float32) * outputs, axis=3)
    dprobs = jnp.concatenate(
        [
            jnp.einsum(
                "bqhd,bgkhd->bhqgk", grad_heads, near_values, preferred_element_type=jnp.float32
            ).reshape(blocks_here, heads_here, BS, near_count),
            jnp.einsum(
                "bqhd,gkhd->bhqgk", grad_heads, far_values, preferred_element_type=jnp.float32
            ).reshape(blocks_here, heads_here, BS, NG * BS),
        ],
        axis=3,
    )
    dscores = probs_full * (dprobs - jnp.transpose(row_dot, (0, 2, 1))[..., None])
    ds_half = dscores.astype(jnp.bfloat16)
    near_ds = ds_half[..., :near_count].reshape(blocks_here, heads_here, BS, near_groups, BS)
    far_ds = ds_half[..., near_count:].reshape(blocks_here, heads_here, BS, NG, BS)
    query_grad = (
        (
            (
                jnp.einsum(
                    "bhqgk,bgkhd->bqhd", near_ds, near_keys, preferred_element_type=jnp.float32
                )
                + jnp.einsum(
                    "bhqgk,gkhd->bqhd", far_ds, far_keys, preferred_element_type=jnp.float32
                )
            )
            * inv_root
        )
        .astype(jnp.bfloat16)
        .reshape(tokens, head_cols)
    )

    def key_value_parts(ds_part, probs_part):
        key_part = (
            jnp.einsum(
                "bhqgk,bqhd->bgkhd", ds_part, query_heads, preferred_element_type=jnp.float32
            )
            * inv_root
        )
        value_part = jnp.einsum(
            "bhqgk,bqhd->bgkhd", probs_part, grad_heads, preferred_element_type=jnp.float32
        )
        out_shape = key_part.shape[:3] + (head_cols,)
        return jnp.concatenate([key_part.reshape(out_shape), value_part.reshape(out_shape)], axis=3)

    random_part = key_value_parts(near_ds[:, :, :, 3:], near_probs[:, :, :, 3:])
    random_part = random_part.astype(jnp.bfloat16).reshape(entries, BS, 2 * head_cols)
    back_rows = (
        jnp.zeros((devices * capacity, BS, 2 * head_cols), jnp.bfloat16)
        .at[my_target]
        .set(random_part)
    )
    arrived = lax.all_to_all(back_rows, "ctx", split_axis=0, concat_axis=0, tiled=True)
    window_part = key_value_parts(near_ds[:, :, :, :3], near_probs[:, :, :, :3])
    zero_block = jnp.zeros((1, BS, 2 * head_cols), jnp.float32)
    own_grad = (
        window_part[:, 1]
        + jnp.concatenate([window_part[1:, 0], zero_block], axis=0)
        + jnp.concatenate([zero_block, window_part[:-1, 2]], axis=0)
    )
    rims_out = jnp.concatenate([window_part[0, 0], window_part[blocks_here - 1, 2]], axis=0)
    rims_in = with_halo(rims_out.astype(jnp.bfloat16), (("ctx", 0),), BS).astype(rims_out.dtype)
    own_grad = own_grad.at[0].add(rims_in[:BS]).at[blocks_here - 1].add(rims_in[3 * BS :])
    far_key = (
        jnp.einsum("bhqgk,bqhd->gkhd", far_ds, query_heads, preferred_element_type=jnp.float32)
        * inv_root
    )
    far_value = jnp.einsum(
        "bhqgk,bqhd->gkhd", far_probs, grad_heads, preferred_element_type=jnp.float32
    )
    far_part = jnp.concatenate(
        [far_key.reshape(NG, BS, head_cols), far_value.reshape(NG, BS, head_cols)], axis=2
    )
    far_sum = all_sum(far_part, "ctx")
    here_ids = jnp.arange(blocks_here, dtype=jnp.int32)
    own_global = (
        (global_owner == my_index)[None, :] & (global_offset[None, :] == here_ids[:, None])
    ).astype(jnp.float32)
    own_grad = own_grad + jnp.einsum(
        "jg,gkc->jkc", own_global, far_sum, precision=lax.Precision.HIGHEST
    )
    weights = (served_used[None, :] & (served_block[None, :] == here_ids[:, None])).astype(
        jnp.bfloat16
    )
    own_grad = own_grad + jnp.einsum(
        "jr,rkc->jkc", weights, arrived, preferred_element_type=jnp.float32
    )
    key_grad = own_grad[..., :head_cols].astype(jnp.bfloat16).reshape(tokens, head_cols)
    value_grad = own_grad[..., head_cols:].astype(jnp.bfloat16).reshape(tokens, head_cols)
    return (query_grad, key_grad, value_grad)


def solution(mesh):
    placed = (
        P(("ctx", "head"), None),
        P(("ctx", "head"), None),
        P(("ctx", "head"), None),
        P(("ctx", "head"), None),
        P(),
        P(),
    )
    return jax.shard_map(
        per_device,
        mesh=mesh,
        in_specs=placed,
        out_specs=(P("ctx", "head"), P("ctx", "head"), P("ctx", "head")),
        check_vma=False,
    )
```

```python
import math

import jax
import numpy as np
import jax.numpy as jnp
from jax import lax
from jax.sharding import PartitionSpec as P

DH = 128
BS = 32
NR = 3
NG = 4


def with_halo(x, axis, order, width):
    ranges = len(order)
    up = [(order[i], order[i + 1]) for i in range(ranges - 1)]
    down = [(j, i) for i, j in up]
    length = x.shape[0]
    before = lax.ppermute(x[length - width :], axis, up)
    after = lax.ppermute(x[:width], axis, down)
    return jnp.concatenate([before, x, after], axis=0)


def chunk_sum(x, axis):
    peers = lax.axis_size(axis)
    parts = lax.all_to_all(x.reshape(peers, -1), axis, split_axis=0, concat_axis=0, tiled=True)
    return jnp.sum(parts.astype(jnp.float32), axis=0)


def chunk_share(chunk, axis, shape, dtype):
    peers = lax.axis_size(axis)
    copies = jnp.broadcast_to(chunk.astype(dtype)[None], (peers,) + chunk.shape)
    return lax.all_to_all(copies, axis, split_axis=0, concat_axis=0, tiled=True).reshape(shape)


def all_sum(x, axis):
    return chunk_share(chunk_sum(x, axis), axis, x.shape, x.dtype)


SEQ_AXES = ("zl", "y", "x")
SWAP_AXES = ("zh", "x")


def swap_places(x):
    side = lax.axis_size("x")
    pairs = [(a * side + b, b * side + a) for a in range(side) for b in range(side)]
    return lax.ppermute(x, SWAP_AXES, pairs)


def per_device(queries, key_states, value_states, out_grad, random_blocks, global_blocks):
    groups = lax.axis_size(("x", "core"))
    rows_in, cols_in = queries.shape
    stacked = jnp.stack([queries, key_states, value_states, out_grad], axis=1)
    stacked = stacked.reshape(rows_in, 4, groups, cols_in // groups)
    stacked = lax.all_to_all(stacked, ("x", "core"), split_axis=2, concat_axis=0, tiled=True)
    stacked = swap_places(stacked)
    query_rows, key_rows, value_rows, grad_rows = (stacked[:, i, 0] for i in range(4))
    tokens = query_rows.shape[0]
    head_cols = query_rows.shape[1]
    heads_here = head_cols // DH
    blocks_here = tokens // BS
    lz, ly, lx = (lax.axis_size(a) for a in SEQ_AXES)
    devices = lz * ly * lx
    my_index = (lax.axis_index("x") * lz + lax.axis_index("zl")) * ly + lax.axis_index("y")
    order = [((r // ly) % lz) * (ly * lx) + (r % ly) * lx + r // (lz * ly) for r in range(devices)]
    range_at = np.argsort(np.array(order)).astype(np.int32)
    slot_of = jnp.array(order, jnp.int32)
    total_blocks = devices * blocks_here
    entries = blocks_here * NR
    capacity = (entries + devices - 1) // devices
    inv_root = 1.0 / math.sqrt(DH)
    kv_rows = jnp.concatenate([key_rows, value_rows], axis=1)
    kv_blocks = kv_rows.reshape(blocks_here, BS, 2 * head_cols)
    extended = with_halo(kv_rows, SEQ_AXES, order, BS)
    extended = extended.reshape(blocks_here + 2, BS, 2 * head_cols)
    window = jnp.stack(
        [extended[:blocks_here], extended[1 : blocks_here + 1], extended[2:]], axis=1
    )
    global_owner = global_blocks // blocks_here
    global_offset = global_blocks % blocks_here
    owned = jnp.take(kv_blocks, global_offset, axis=0)
    owned = jnp.where((global_owner == my_index)[:, None, None], owned, jnp.zeros_like(owned))
    global_kv = all_sum(owned, SEQ_AXES)
    entry_table = random_blocks.reshape(devices, entries)
    table_owner = entry_table // blocks_here
    table_offset = entry_table % blocks_here
    positions = jnp.arange(entries, dtype=jnp.int32)
    before = positions[None, :] < positions[:, None]
    matches = (table_owner[:, :, None] == table_owner[:, None, :]) & before[None]
    table_slot = jnp.sum(matches.astype(jnp.int32), axis=2)
    my_owner = lax.dynamic_index_in_dim(table_owner, my_index, 0, keepdims=False)
    my_slot = lax.dynamic_index_in_dim(table_slot, my_index, 0, keepdims=False)
    my_target = slot_of[my_owner] * capacity + my_slot
    slot_ids = jnp.arange(capacity, dtype=jnp.int32)
    served = (table_owner == my_index)[:, :, None] & (
        table_slot[:, :, None] == slot_ids[None, None, :]
    )
    served_block = jnp.sum(jnp.where(served, table_offset[:, :, None], 0), axis=1)[range_at].reshape(-1)
    served_used = jnp.any(served, axis=1)[range_at].reshape(-1)
    outgoing = jnp.take(kv_blocks, served_block, axis=0)
    incoming = lax.all_to_all(outgoing, SEQ_AXES, split_axis=0, concat_axis=0, tiled=True)
    fetched = jnp.take(incoming, my_target, axis=0).reshape(blocks_here, NR, BS, 2 * head_cols)
    near_kv = jnp.concatenate([window, fetched], axis=1)
    near_groups = 3 + NR
    near_count = near_groups * BS
    query_heads = query_rows.reshape(blocks_here, BS, heads_here, DH)
    grad_heads = grad_rows.reshape(blocks_here, BS, heads_here, DH)
    near_keys = near_kv[..., :head_cols].reshape(blocks_here, near_groups, BS, heads_here, DH)
    near_values = near_kv[..., head_cols:].reshape(blocks_here, near_groups, BS, heads_here, DH)
    far_keys = global_kv[..., :head_cols].reshape(NG, BS, heads_here, DH)
    far_values = global_kv[..., head_cols:].reshape(NG, BS, heads_here, DH)
    scores = (
        jnp.concatenate(
            [
                jnp.einsum(
                    "bqhd,bgkhd->bhqgk", query_heads, near_keys, preferred_element_type=jnp.float32
                ).reshape(blocks_here, heads_here, BS, near_count),
                jnp.einsum(
                    "bqhd,gkhd->bhqgk", query_heads, far_keys, preferred_element_type=jnp.float32
                ).reshape(blocks_here, heads_here, BS, NG * BS),
            ],
            axis=3,
        )
        * inv_root
    )
    block_ids = my_index * blocks_here + jnp.arange(blocks_here, dtype=jnp.int32)
    usable = jnp.concatenate(
        [
            (block_ids > 0)[:, None],
            jnp.ones((blocks_here, 1), bool),
            (block_ids < total_blocks - 1)[:, None],
            jnp.ones((blocks_here, NR + NG), bool),
        ],
        axis=1,
    )
    column_ok = jnp.repeat(usable, BS, axis=1)[:, None, None, :]
    masked = jnp.where(column_ok, scores, -jnp.inf)
    row_max = jnp.max(masked, axis=3, keepdims=True)
    log_total = row_max + jnp.log(jnp.sum(jnp.exp(masked - row_max), axis=3, keepdims=True))
    probs_full = jnp.exp(masked - log_total)
    probs_half = probs_full.astype(jnp.bfloat16)
    near_probs = probs_half[..., :near_count].reshape(blocks_here, heads_here, BS, near_groups, BS)
    far_probs = probs_half[..., near_count:].reshape(blocks_here, heads_here, BS, NG, BS)
    outputs = jnp.einsum(
        "bhqgk,bgkhd->bqhd", near_probs, near_values, preferred_element_type=jnp.float32
    ) + jnp.einsum("bhqgk,gkhd->bqhd", far_probs, far_values, preferred_element_type=jnp.float32)
    row_dot = jnp.sum(grad_heads.astype(jnp.float32) * outputs, axis=3)
    dprobs = jnp.concatenate(
        [
            jnp.einsum(
                "bqhd,bgkhd->bhqgk", grad_heads, near_values, preferred_element_type=jnp.float32
            ).reshape(blocks_here, heads_here, BS, near_count),
            jnp.einsum(
                "bqhd,gkhd->bhqgk", grad_heads, far_values, preferred_element_type=jnp.float32
            ).reshape(blocks_here, heads_here, BS, NG * BS),
        ],
        axis=3,
    )
    dscores = probs_full * (dprobs - jnp.transpose(row_dot, (0, 2, 1))[..., None])
    ds_half = dscores.astype(jnp.bfloat16)
    near_ds = ds_half[..., :near_count].reshape(blocks_here, heads_here, BS, near_groups, BS)
    far_ds = ds_half[..., near_count:].reshape(blocks_here, heads_here, BS, NG, BS)
    query_grad = (
        (
            (
                jnp.einsum(
                    "bhqgk,bgkhd->bqhd", near_ds, near_keys, preferred_element_type=jnp.float32
                )
                + jnp.einsum(
                    "bhqgk,gkhd->bqhd", far_ds, far_keys, preferred_element_type=jnp.float32
                )
            )
            * inv_root
        )
        .astype(jnp.bfloat16)
        .reshape(tokens, head_cols)
    )

    def key_value_parts(ds_part, probs_part):
        key_part = (
            jnp.einsum(
                "bhqgk,bqhd->bgkhd", ds_part, query_heads, preferred_element_type=jnp.float32
            )
            * inv_root
        )
        value_part = jnp.einsum(
            "bhqgk,bqhd->bgkhd", probs_part, grad_heads, preferred_element_type=jnp.float32
        )
        out_shape = key_part.shape[:3] + (head_cols,)
        return jnp.concatenate([key_part.reshape(out_shape), value_part.reshape(out_shape)], axis=3)

    random_part = key_value_parts(near_ds[:, :, :, 3:], near_probs[:, :, :, 3:])
    random_part = random_part.astype(jnp.bfloat16).reshape(entries, BS, 2 * head_cols)
    back_rows = (
        jnp.zeros((devices * capacity, BS, 2 * head_cols), jnp.bfloat16)
        .at[my_target]
        .set(random_part)
    )
    arrived = lax.all_to_all(back_rows, SEQ_AXES, split_axis=0, concat_axis=0, tiled=True)
    window_part = key_value_parts(near_ds[:, :, :, :3], near_probs[:, :, :, :3])
    zero_block = jnp.zeros((1, BS, 2 * head_cols), jnp.float32)
    own_grad = (
        window_part[:, 1]
        + jnp.concatenate([window_part[1:, 0], zero_block], axis=0)
        + jnp.concatenate([zero_block, window_part[:-1, 2]], axis=0)
    )
    rims_out = jnp.concatenate([window_part[0, 0], window_part[blocks_here - 1, 2]], axis=0)
    rims_in = with_halo(rims_out.astype(jnp.bfloat16), SEQ_AXES, order, BS).astype(rims_out.dtype)
    own_grad = own_grad.at[0].add(rims_in[:BS]).at[blocks_here - 1].add(rims_in[3 * BS :])
    far_key = (
        jnp.einsum("bhqgk,bqhd->gkhd", far_ds, query_heads, preferred_element_type=jnp.float32)
        * inv_root
    )
    far_value = jnp.einsum(
        "bhqgk,bqhd->gkhd", far_probs, grad_heads, preferred_element_type=jnp.float32
    )
    far_part = jnp.concatenate(
        [far_key.reshape(NG, BS, head_cols), far_value.reshape(NG, BS, head_cols)], axis=2
    )
    far_sum = all_sum(far_part, SEQ_AXES)
    here_ids = jnp.arange(blocks_here, dtype=jnp.int32)
    own_global = (
        (global_owner == my_index)[None, :] & (global_offset[None, :] == here_ids[:, None])
    ).astype(jnp.float32)
    own_grad = own_grad + jnp.einsum(
        "jg,gkc->jkc", own_global, far_sum, precision=lax.Precision.HIGHEST
    )
    weights = (served_used[None, :] & (served_block[None, :] == here_ids[:, None])).astype(
        jnp.bfloat16
    )
    own_grad = own_grad + jnp.einsum(
        "jr,rkc->jkc", weights, arrived, preferred_element_type=jnp.float32
    )
    key_grad = own_grad[..., :head_cols].astype(jnp.bfloat16).reshape(tokens, head_cols)
    value_grad = own_grad[..., head_cols:].astype(jnp.bfloat16).reshape(tokens, head_cols)
    return tuple(swap_places(out) for out in (query_grad, key_grad, value_grad))


def solution(mesh):
    side = mesh.devices.shape[1] // 2
    grid = mesh.devices.reshape(-1, mesh.devices.shape[0] // (side * side), side, side, 2)
    cube = jax.sharding.Mesh(grid, ("zh", "zl", "y", "x", "core"))
    rows = ("zh", "zl", "y", "x", "core")
    placed = (P(rows, None),) * 4 + (P(), P())
    out = P(("zh", "zl", "y"), ("x", "core"))
    return jax.shard_map(
        per_device,
        mesh=cube,
        in_specs=placed,
        out_specs=(out, out, out),
        check_vma=False,
    )
```

```python
import math

import jax
import numpy as np
import jax.numpy as jnp
from jax import lax
from jax.sharding import PartitionSpec as P

DH = 128
BS = 32
NR = 3
NG = 4


def with_halo(x, axis, order, width):
    ranges = len(order)
    up = [(order[i], order[i + 1]) for i in range(ranges - 1)]
    down = [(j, i) for i, j in up]
    length = x.shape[0]
    before = lax.ppermute(x[length - width :], axis, up)
    after = lax.ppermute(x[:width], axis, down)
    return jnp.concatenate([before, x, after], axis=0)


def chunk_sum(x, axis):
    peers = lax.axis_size(axis)
    parts = lax.all_to_all(x.reshape(peers, -1), axis, split_axis=0, concat_axis=0, tiled=True)
    return jnp.sum(parts.astype(jnp.float32), axis=0)


def chunk_share(chunk, axis, shape, dtype):
    peers = lax.axis_size(axis)
    copies = jnp.broadcast_to(chunk.astype(dtype)[None], (peers,) + chunk.shape)
    return lax.all_to_all(copies, axis, split_axis=0, concat_axis=0, tiled=True).reshape(shape)


def all_sum(x, axis):
    return chunk_share(chunk_sum(x, axis), axis, x.shape, x.dtype)


SEQ_AXES = ("zl", "y", "x")
SWAP_AXES = ("zh", "x")


def swap_places(x):
    side = lax.axis_size("x")
    pairs = [(a * side + b, b * side + a) for a in range(side) for b in range(side)]
    return lax.ppermute(x, SWAP_AXES, pairs)


def per_device(queries, key_states, value_states, out_grad, random_blocks, global_blocks):
    groups = lax.axis_size(("x", "core"))
    rows_in, cols_in = queries.shape
    stacked = jnp.stack([queries, key_states, value_states, out_grad], axis=1)
    stacked = stacked.reshape(rows_in, 4, groups, cols_in // groups)
    stacked = lax.all_to_all(stacked, ("x", "core"), split_axis=2, concat_axis=0, tiled=True)
    stacked = swap_places(stacked)
    query_rows, key_rows, value_rows, grad_rows = (stacked[:, i, 0] for i in range(4))
    tokens = query_rows.shape[0]
    head_cols = query_rows.shape[1]
    heads_here = head_cols // DH
    blocks_here = tokens // BS
    lz, ly, lx = (lax.axis_size(a) for a in SEQ_AXES)
    devices = lz * ly * lx
    my_index = (lax.axis_index("x") * lz + lax.axis_index("zl")) * ly + lax.axis_index("y")
    order = [((r // ly) % lz) * (ly * lx) + (r % ly) * lx + r // (lz * ly) for r in range(devices)]
    range_at = np.argsort(np.array(order)).astype(np.int32)
    slot_of = jnp.array(order, jnp.int32)
    total_blocks = devices * blocks_here
    entries = blocks_here * NR
    capacity = (entries + devices - 1) // devices
    inv_root = 1.0 / math.sqrt(DH)
    kv_rows = jnp.concatenate([key_rows, value_rows], axis=1)
    kv_blocks = kv_rows.reshape(blocks_here, BS, 2 * head_cols)
    extended = with_halo(kv_rows, SEQ_AXES, order, BS)
    extended = extended.reshape(blocks_here + 2, BS, 2 * head_cols)
    window = jnp.stack(
        [extended[:blocks_here], extended[1 : blocks_here + 1], extended[2:]], axis=1
    )
    global_owner = global_blocks // blocks_here
    global_offset = global_blocks % blocks_here
    owned = jnp.take(kv_blocks, global_offset, axis=0)
    owned = jnp.where((global_owner == my_index)[:, None, None], owned, jnp.zeros_like(owned))
    entry_table = random_blocks.reshape(devices, entries)
    table_owner = entry_table // blocks_here
    table_offset = entry_table % blocks_here
    positions = jnp.arange(entries, dtype=jnp.int32)
    before = positions[None, :] < positions[:, None]
    matches = (table_owner[:, :, None] == table_owner[:, None, :]) & before[None]
    table_slot = jnp.sum(matches.astype(jnp.int32), axis=2)
    my_owner = lax.dynamic_index_in_dim(table_owner, my_index, 0, keepdims=False)
    my_slot = lax.dynamic_index_in_dim(table_slot, my_index, 0, keepdims=False)
    my_target = slot_of[my_owner] * capacity + my_slot
    slot_ids = jnp.arange(capacity, dtype=jnp.int32)
    served = (table_owner == my_index)[:, :, None] & (
        table_slot[:, :, None] == slot_ids[None, None, :]
    )
    served_block = jnp.sum(jnp.where(served, table_offset[:, :, None], 0), axis=1)[range_at].reshape(-1)
    served_used = jnp.any(served, axis=1)[range_at].reshape(-1)
    outgoing = jnp.take(kv_blocks, served_block, axis=0)
    owned_parts = owned.reshape(devices, -1, 2 * head_cols)
    slot_rows = capacity * BS
    outgoing = outgoing.reshape(devices, slot_rows, 2 * head_cols)
    outgoing = jnp.concatenate([outgoing, owned_parts], axis=1)
    incoming = lax.all_to_all(outgoing, SEQ_AXES, split_axis=0, concat_axis=0, tiled=True)
    global_chunk = jnp.sum(incoming[:, slot_rows:].astype(jnp.float32), axis=0)
    global_kv = chunk_share(global_chunk, SEQ_AXES, owned.shape, owned.dtype)
    incoming = incoming[:, :slot_rows].reshape(devices * capacity, BS, 2 * head_cols)
    fetched = jnp.take(incoming, my_target, axis=0).reshape(blocks_here, NR, BS, 2 * head_cols)
    near_kv = jnp.concatenate([window, fetched], axis=1)
    near_groups = 3 + NR
    near_count = near_groups * BS
    query_heads = query_rows.reshape(blocks_here, BS, heads_here, DH)
    grad_heads = grad_rows.reshape(blocks_here, BS, heads_here, DH)
    near_keys = near_kv[..., :head_cols].reshape(blocks_here, near_groups, BS, heads_here, DH)
    near_values = near_kv[..., head_cols:].reshape(blocks_here, near_groups, BS, heads_here, DH)
    far_keys = global_kv[..., :head_cols].reshape(NG, BS, heads_here, DH)
    far_values = global_kv[..., head_cols:].reshape(NG, BS, heads_here, DH)
    scores = (
        jnp.concatenate(
            [
                jnp.einsum(
                    "bqhd,bgkhd->bhqgk", query_heads, near_keys, preferred_element_type=jnp.float32
                ).reshape(blocks_here, heads_here, BS, near_count),
                jnp.einsum(
                    "bqhd,gkhd->bhqgk", query_heads, far_keys, preferred_element_type=jnp.float32
                ).reshape(blocks_here, heads_here, BS, NG * BS),
            ],
            axis=3,
        )
        * inv_root
    )
    block_ids = my_index * blocks_here + jnp.arange(blocks_here, dtype=jnp.int32)
    usable = jnp.concatenate(
        [
            (block_ids > 0)[:, None],
            jnp.ones((blocks_here, 1), bool),
            (block_ids < total_blocks - 1)[:, None],
            jnp.ones((blocks_here, NR + NG), bool),
        ],
        axis=1,
    )
    column_ok = jnp.repeat(usable, BS, axis=1)[:, None, None, :]
    masked = jnp.where(column_ok, scores, -jnp.inf)
    row_max = jnp.max(masked, axis=3, keepdims=True)
    log_total = row_max + jnp.log(jnp.sum(jnp.exp(masked - row_max), axis=3, keepdims=True))
    probs_full = jnp.exp(masked - log_total)
    probs_half = probs_full.astype(jnp.bfloat16)
    near_probs = probs_half[..., :near_count].reshape(blocks_here, heads_here, BS, near_groups, BS)
    far_probs = probs_half[..., near_count:].reshape(blocks_here, heads_here, BS, NG, BS)
    outputs = jnp.einsum(
        "bhqgk,bgkhd->bqhd", near_probs, near_values, preferred_element_type=jnp.float32
    ) + jnp.einsum("bhqgk,gkhd->bqhd", far_probs, far_values, preferred_element_type=jnp.float32)
    row_dot = jnp.sum(grad_heads.astype(jnp.float32) * outputs, axis=3)
    dprobs = jnp.concatenate(
        [
            jnp.einsum(
                "bqhd,bgkhd->bhqgk", grad_heads, near_values, preferred_element_type=jnp.float32
            ).reshape(blocks_here, heads_here, BS, near_count),
            jnp.einsum(
                "bqhd,gkhd->bhqgk", grad_heads, far_values, preferred_element_type=jnp.float32
            ).reshape(blocks_here, heads_here, BS, NG * BS),
        ],
        axis=3,
    )
    dscores = probs_full * (dprobs - jnp.transpose(row_dot, (0, 2, 1))[..., None])
    ds_half = dscores.astype(jnp.bfloat16)
    near_ds = ds_half[..., :near_count].reshape(blocks_here, heads_here, BS, near_groups, BS)
    far_ds = ds_half[..., near_count:].reshape(blocks_here, heads_here, BS, NG, BS)
    query_grad = (
        (
            (
                jnp.einsum(
                    "bhqgk,bgkhd->bqhd", near_ds, near_keys, preferred_element_type=jnp.float32
                )
                + jnp.einsum(
                    "bhqgk,gkhd->bqhd", far_ds, far_keys, preferred_element_type=jnp.float32
                )
            )
            * inv_root
        )
        .astype(jnp.bfloat16)
        .reshape(tokens, head_cols)
    )

    def key_value_parts(ds_part, probs_part):
        key_part = (
            jnp.einsum(
                "bhqgk,bqhd->bgkhd", ds_part, query_heads, preferred_element_type=jnp.float32
            )
            * inv_root
        )
        value_part = jnp.einsum(
            "bhqgk,bqhd->bgkhd", probs_part, grad_heads, preferred_element_type=jnp.float32
        )
        out_shape = key_part.shape[:3] + (head_cols,)
        return jnp.concatenate([key_part.reshape(out_shape), value_part.reshape(out_shape)], axis=3)

    random_part = key_value_parts(near_ds[:, :, :, 3:], near_probs[:, :, :, 3:])
    random_part = random_part.astype(jnp.bfloat16).reshape(entries, BS, 2 * head_cols)
    back_rows = (
        jnp.zeros((devices * capacity, BS, 2 * head_cols), jnp.bfloat16)
        .at[my_target]
        .set(random_part)
    )
    arrived = lax.all_to_all(back_rows, SEQ_AXES, split_axis=0, concat_axis=0, tiled=True)
    window_part = key_value_parts(near_ds[:, :, :, :3], near_probs[:, :, :, :3])
    zero_block = jnp.zeros((1, BS, 2 * head_cols), jnp.float32)
    own_grad = (
        window_part[:, 1]
        + jnp.concatenate([window_part[1:, 0], zero_block], axis=0)
        + jnp.concatenate([zero_block, window_part[:-1, 2]], axis=0)
    )
    rims_out = jnp.concatenate([window_part[0, 0], window_part[blocks_here - 1, 2]], axis=0)
    rims_in = with_halo(rims_out.astype(jnp.bfloat16), SEQ_AXES, order, BS).astype(rims_out.dtype)
    own_grad = own_grad.at[0].add(rims_in[:BS]).at[blocks_here - 1].add(rims_in[3 * BS :])
    far_key = (
        jnp.einsum("bhqgk,bqhd->gkhd", far_ds, query_heads, preferred_element_type=jnp.float32)
        * inv_root
    )
    far_value = jnp.einsum(
        "bhqgk,bqhd->gkhd", far_probs, grad_heads, preferred_element_type=jnp.float32
    )
    far_part = jnp.concatenate(
        [far_key.reshape(NG, BS, head_cols), far_value.reshape(NG, BS, head_cols)], axis=2
    )
    far_sum = all_sum(far_part, SEQ_AXES)
    here_ids = jnp.arange(blocks_here, dtype=jnp.int32)
    own_global = (
        (global_owner == my_index)[None, :] & (global_offset[None, :] == here_ids[:, None])
    ).astype(jnp.float32)
    own_grad = own_grad + jnp.einsum(
        "jg,gkc->jkc", own_global, far_sum, precision=lax.Precision.HIGHEST
    )
    weights = (served_used[None, :] & (served_block[None, :] == here_ids[:, None])).astype(
        jnp.bfloat16
    )
    own_grad = own_grad + jnp.einsum(
        "jr,rkc->jkc", weights, arrived, preferred_element_type=jnp.float32
    )
    key_grad = own_grad[..., :head_cols].astype(jnp.bfloat16).reshape(tokens, head_cols)
    value_grad = own_grad[..., head_cols:].astype(jnp.bfloat16).reshape(tokens, head_cols)
    outs = swap_places(jnp.stack([query_grad, key_grad, value_grad]))
    return outs[0], outs[1], outs[2]


def solution(mesh):
    side = mesh.devices.shape[1] // 2
    grid = mesh.devices.reshape(-1, mesh.devices.shape[0] // (side * side), side, side, 2)
    cube = jax.sharding.Mesh(grid, ("zh", "zl", "y", "x", "core"))
    rows = ("zh", "zl", "y", "x", "core")
    placed = (P(rows, None),) * 4 + (P(), P())
    out = P(("zh", "zl", "y"), ("x", "core"))
    return jax.shard_map(
        per_device,
        mesh=cube,
        in_specs=placed,
        out_specs=(out, out, out),
        check_vma=False,
    )
```

```python
import math

import jax
import numpy as np
import jax.numpy as jnp
from jax import lax
from jax.sharding import PartitionSpec as P

DH = 128
BS = 32
NR = 3
NG = 4


def with_halo(x, axis, order, width):
    ranges = len(order)
    up = [(order[i], order[i + 1]) for i in range(ranges - 1)]
    down = [(j, i) for i, j in up]
    length = x.shape[0]
    before = lax.ppermute(x[length - width :], axis, up)
    after = lax.ppermute(x[:width], axis, down)
    return jnp.concatenate([before, x, after], axis=0)


def chunk_sum(x, axis):
    peers = lax.axis_size(axis)
    parts = lax.all_to_all(x.reshape(peers, -1), axis, split_axis=0, concat_axis=0, tiled=True)
    return jnp.sum(parts.astype(jnp.float32), axis=0)


def chunk_share(chunk, axis, shape, dtype):
    peers = lax.axis_size(axis)
    copies = jnp.broadcast_to(chunk.astype(dtype)[None], (peers,) + chunk.shape)
    return lax.all_to_all(copies, axis, split_axis=0, concat_axis=0, tiled=True).reshape(shape)


def all_sum(x, axis):
    return chunk_share(chunk_sum(x, axis), axis, x.shape, x.dtype)


SEQ_AXES = ("zl", "y", "x")
SWAP_AXES = ("zh", "x")


def swap_places(x):
    side = lax.axis_size("x")
    pairs = [(a * side + b, b * side + a) for a in range(side) for b in range(side)]
    return lax.ppermute(x, SWAP_AXES, pairs)


def per_device(queries, key_states, value_states, out_grad, random_blocks, global_blocks):
    groups = lax.axis_size(("x", "core"))
    rows_in, cols_in = queries.shape
    stacked = jnp.stack([queries, key_states, value_states, out_grad], axis=1)
    stacked = stacked.reshape(rows_in, 4, groups, cols_in // groups)
    stacked = lax.all_to_all(stacked, ("x", "core"), split_axis=2, concat_axis=0, tiled=True)
    stacked = swap_places(stacked)
    query_rows, key_rows, value_rows, grad_rows = (stacked[:, i, 0] for i in range(4))
    tokens = query_rows.shape[0]
    head_cols = query_rows.shape[1]
    heads_here = head_cols // DH
    blocks_here = tokens // BS
    lz, ly, lx = (lax.axis_size(a) for a in SEQ_AXES)
    devices = lz * ly * lx
    my_index = (lax.axis_index("x") * lz + lax.axis_index("zl")) * ly + lax.axis_index("y")
    order = [((r // ly) % lz) * (ly * lx) + (r % ly) * lx + r // (lz * ly) for r in range(devices)]
    range_at = np.argsort(np.array(order)).astype(np.int32)
    slot_of = jnp.array(order, jnp.int32)
    total_blocks = devices * blocks_here
    entries = blocks_here * NR
    capacity = (entries + devices - 1) // devices
    inv_root = 1.0 / math.sqrt(DH)
    kv_rows = jnp.concatenate([key_rows, value_rows], axis=1)
    kv_blocks = kv_rows.reshape(blocks_here, BS, 2 * head_cols)
    extended = with_halo(kv_rows, SEQ_AXES, order, BS)
    extended = extended.reshape(blocks_here + 2, BS, 2 * head_cols)
    window = jnp.stack(
        [extended[:blocks_here], extended[1 : blocks_here + 1], extended[2:]], axis=1
    )
    global_owner = global_blocks // blocks_here
    global_offset = global_blocks % blocks_here
    owned = jnp.take(kv_blocks, global_offset, axis=0)
    owned = jnp.where((global_owner == my_index)[:, None, None], owned, jnp.zeros_like(owned))
    entry_table = random_blocks.reshape(devices, entries)
    table_owner = entry_table // blocks_here
    table_offset = entry_table % blocks_here
    positions = jnp.arange(entries, dtype=jnp.int32)
    before = positions[None, :] < positions[:, None]
    matches = (table_owner[:, :, None] == table_owner[:, None, :]) & before[None]
    table_slot = jnp.sum(matches.astype(jnp.int32), axis=2)
    my_owner = lax.dynamic_index_in_dim(table_owner, my_index, 0, keepdims=False)
    my_slot = lax.dynamic_index_in_dim(table_slot, my_index, 0, keepdims=False)
    my_target = slot_of[my_owner] * capacity + my_slot
    slot_ids = jnp.arange(capacity, dtype=jnp.int32)
    served = (table_owner == my_index)[:, :, None] & (
        table_slot[:, :, None] == slot_ids[None, None, :]
    )
    served_block = jnp.sum(jnp.where(served, table_offset[:, :, None], 0), axis=1)[range_at].reshape(-1)
    served_used = jnp.any(served, axis=1)[range_at].reshape(-1)
    outgoing = jnp.take(kv_blocks, served_block, axis=0)
    owned_parts = owned.reshape(devices, -1, 2 * head_cols)
    slot_rows = capacity * BS
    slot_size = slot_rows * 2 * head_cols
    outgoing = jnp.concatenate(
        [outgoing.reshape(devices, slot_size), owned_parts.reshape(devices, -1)], axis=1
    )
    incoming = lax.all_to_all(outgoing, SEQ_AXES, split_axis=0, concat_axis=0, tiled=True)
    global_chunk = jnp.sum(incoming[:, slot_size:].astype(jnp.float32), axis=0)
    global_kv = chunk_share(global_chunk, SEQ_AXES, owned.shape, owned.dtype)
    incoming = incoming[:, :slot_size].reshape(devices * capacity, BS, 2 * head_cols)
    fetched = jnp.take(incoming, my_target, axis=0).reshape(blocks_here, NR, BS, 2 * head_cols)
    near_kv = jnp.concatenate([window, fetched], axis=1)
    near_groups = 3 + NR
    near_count = near_groups * BS
    query_heads = query_rows.reshape(blocks_here, BS, heads_here, DH)
    grad_heads = grad_rows.reshape(blocks_here, BS, heads_here, DH)
    near_keys = near_kv[..., :head_cols].reshape(blocks_here, near_groups, BS, heads_here, DH)
    near_values = near_kv[..., head_cols:].reshape(blocks_here, near_groups, BS, heads_here, DH)
    far_keys = global_kv[..., :head_cols].reshape(NG, BS, heads_here, DH)
    far_values = global_kv[..., head_cols:].reshape(NG, BS, heads_here, DH)
    scores = (
        jnp.concatenate(
            [
                jnp.einsum(
                    "bqhd,bgkhd->bhqgk", query_heads, near_keys, preferred_element_type=jnp.float32
                ).reshape(blocks_here, heads_here, BS, near_count),
                jnp.einsum(
                    "bqhd,gkhd->bhqgk", query_heads, far_keys, preferred_element_type=jnp.float32
                ).reshape(blocks_here, heads_here, BS, NG * BS),
            ],
            axis=3,
        )
        * inv_root
    )
    block_ids = my_index * blocks_here + jnp.arange(blocks_here, dtype=jnp.int32)
    usable = jnp.concatenate(
        [
            (block_ids > 0)[:, None],
            jnp.ones((blocks_here, 1), bool),
            (block_ids < total_blocks - 1)[:, None],
            jnp.ones((blocks_here, NR + NG), bool),
        ],
        axis=1,
    )
    column_ok = jnp.repeat(usable, BS, axis=1)[:, None, None, :]
    masked = jnp.where(column_ok, scores, -jnp.inf)
    row_max = jnp.max(masked, axis=3, keepdims=True)
    log_total = row_max + jnp.log(jnp.sum(jnp.exp(masked - row_max), axis=3, keepdims=True))
    probs_full = jnp.exp(masked - log_total)
    probs_half = probs_full.astype(jnp.bfloat16)
    near_probs = probs_half[..., :near_count].reshape(blocks_here, heads_here, BS, near_groups, BS)
    far_probs = probs_half[..., near_count:].reshape(blocks_here, heads_here, BS, NG, BS)
    outputs = jnp.einsum(
        "bhqgk,bgkhd->bqhd", near_probs, near_values, preferred_element_type=jnp.float32
    ) + jnp.einsum("bhqgk,gkhd->bqhd", far_probs, far_values, preferred_element_type=jnp.float32)
    row_dot = jnp.sum(grad_heads.astype(jnp.float32) * outputs, axis=3)
    dprobs = jnp.concatenate(
        [
            jnp.einsum(
                "bqhd,bgkhd->bhqgk", grad_heads, near_values, preferred_element_type=jnp.float32
            ).reshape(blocks_here, heads_here, BS, near_count),
            jnp.einsum(
                "bqhd,gkhd->bhqgk", grad_heads, far_values, preferred_element_type=jnp.float32
            ).reshape(blocks_here, heads_here, BS, NG * BS),
        ],
        axis=3,
    )
    dscores = probs_full * (dprobs - jnp.transpose(row_dot, (0, 2, 1))[..., None])
    ds_half = dscores.astype(jnp.bfloat16)
    near_ds = ds_half[..., :near_count].reshape(blocks_here, heads_here, BS, near_groups, BS)
    far_ds = ds_half[..., near_count:].reshape(blocks_here, heads_here, BS, NG, BS)
    query_grad = (
        (
            (
                jnp.einsum(
                    "bhqgk,bgkhd->bqhd", near_ds, near_keys, preferred_element_type=jnp.float32
                )
                + jnp.einsum(
                    "bhqgk,gkhd->bqhd", far_ds, far_keys, preferred_element_type=jnp.float32
                )
            )
            * inv_root
        )
        .astype(jnp.bfloat16)
        .reshape(tokens, head_cols)
    )

    def key_value_parts(ds_part, probs_part):
        key_part = (
            jnp.einsum(
                "bhqgk,bqhd->bgkhd", ds_part, query_heads, preferred_element_type=jnp.float32
            )
            * inv_root
        )
        value_part = jnp.einsum(
            "bhqgk,bqhd->bgkhd", probs_part, grad_heads, preferred_element_type=jnp.float32
        )
        out_shape = key_part.shape[:3] + (head_cols,)
        return jnp.concatenate([key_part.reshape(out_shape), value_part.reshape(out_shape)], axis=3)

    random_part = key_value_parts(near_ds[:, :, :, 3:], near_probs[:, :, :, 3:])
    random_part = random_part.astype(jnp.bfloat16).reshape(entries, BS, 2 * head_cols)
    back_rows = (
        jnp.zeros((devices * capacity, BS, 2 * head_cols), jnp.bfloat16)
        .at[my_target]
        .set(random_part)
    )
    arrived = lax.all_to_all(back_rows, SEQ_AXES, split_axis=0, concat_axis=0, tiled=True)
    window_part = key_value_parts(near_ds[:, :, :, :3], near_probs[:, :, :, :3])
    zero_block = jnp.zeros((1, BS, 2 * head_cols), jnp.float32)
    own_grad = (
        window_part[:, 1]
        + jnp.concatenate([window_part[1:, 0], zero_block], axis=0)
        + jnp.concatenate([zero_block, window_part[:-1, 2]], axis=0)
    )
    rims_out = jnp.concatenate([window_part[0, 0], window_part[blocks_here - 1, 2]], axis=0)
    rims_in = with_halo(rims_out.astype(jnp.bfloat16), SEQ_AXES, order, BS).astype(rims_out.dtype)
    own_grad = own_grad.at[0].add(rims_in[:BS]).at[blocks_here - 1].add(rims_in[3 * BS :])
    far_key = (
        jnp.einsum("bhqgk,bqhd->gkhd", far_ds, query_heads, preferred_element_type=jnp.float32)
        * inv_root
    )
    far_value = jnp.einsum(
        "bhqgk,bqhd->gkhd", far_probs, grad_heads, preferred_element_type=jnp.float32
    )
    far_part = jnp.concatenate(
        [far_key.reshape(NG, BS, head_cols), far_value.reshape(NG, BS, head_cols)], axis=2
    )
    far_sum = all_sum(far_part, SEQ_AXES)
    here_ids = jnp.arange(blocks_here, dtype=jnp.int32)
    own_global = (
        (global_owner == my_index)[None, :] & (global_offset[None, :] == here_ids[:, None])
    ).astype(jnp.float32)
    own_grad = own_grad + jnp.einsum(
        "jg,gkc->jkc", own_global, far_sum, precision=lax.Precision.HIGHEST
    )
    weights = (served_used[None, :] & (served_block[None, :] == here_ids[:, None])).astype(
        jnp.bfloat16
    )
    own_grad = own_grad + jnp.einsum(
        "jr,rkc->jkc", weights, arrived, preferred_element_type=jnp.float32
    )
    key_grad = own_grad[..., :head_cols].astype(jnp.bfloat16).reshape(tokens, head_cols)
    value_grad = own_grad[..., head_cols:].astype(jnp.bfloat16).reshape(tokens, head_cols)
    outs = swap_places(jnp.stack([query_grad, key_grad, value_grad]))
    return outs[0], outs[1], outs[2]


def solution(mesh):
    side = mesh.devices.shape[1] // 2
    grid = mesh.devices.reshape(-1, mesh.devices.shape[0] // (side * side), side, side, 2)
    cube = jax.sharding.Mesh(grid, ("zh", "zl", "y", "x", "core"))
    rows = ("zh", "zl", "y", "x", "core")
    placed = (P(rows, None),) * 4 + (P(), P())
    out = P(("zh", "zl", "y"), ("x", "core"))
    return jax.shard_map(
        per_device,
        mesh=cube,
        in_specs=placed,
        out_specs=(out, out, out),
        check_vma=False,
    )
```

```python
import math

import jax
import numpy as np
import jax.numpy as jnp
from jax import lax
from jax.sharding import PartitionSpec as P

DH = 128
BS = 32
NR = 3
NG = 4


def with_halo(x, axis, order, width):
    ranges = len(order)
    up = [(order[i], order[i + 1]) for i in range(ranges - 1)]
    down = [(j, i) for i, j in up]
    length = x.shape[0]
    before = lax.ppermute(x[length - width :], axis, up)
    after = lax.ppermute(x[:width], axis, down)
    return jnp.concatenate([before, x, after], axis=0)


def chunk_sum(x, axis):
    peers = lax.axis_size(axis)
    parts = lax.all_to_all(x.reshape(peers, -1), axis, split_axis=0, concat_axis=0, tiled=True)
    return jnp.sum(parts.astype(jnp.float32), axis=0)


def chunk_share(chunk, axis, shape, dtype):
    peers = lax.axis_size(axis)
    copies = jnp.broadcast_to(chunk.astype(dtype)[None], (peers,) + chunk.shape)
    return lax.all_to_all(copies, axis, split_axis=0, concat_axis=0, tiled=True).reshape(shape)


def all_sum(x, axis):
    return chunk_share(chunk_sum(x, axis), axis, x.shape, x.dtype)


SEQ_AXES = ("zl", "y", "x")
SWAP_AXES = ("zh", "x")


def swap_places(x):
    side = lax.axis_size("x")
    pairs = [(a * side + b, b * side + a) for a in range(side) for b in range(side)]
    return lax.ppermute(x, SWAP_AXES, pairs)


def per_device(queries, key_states, value_states, out_grad, random_blocks, global_blocks):
    groups = lax.axis_size(("x", "core"))
    rows_in, cols_in = queries.shape
    stacked = jnp.stack([queries, key_states, value_states, out_grad], axis=1)
    stacked = stacked.reshape(rows_in, 4, groups, cols_in // groups)
    stacked = lax.all_to_all(stacked, ("x", "core"), split_axis=2, concat_axis=0, tiled=True)
    home_index = lax.axis_index(("zh", "zl", "y"))
    home_blocks = stacked.shape[0] // BS
    home_kv = jnp.concatenate([stacked[:, 1, 0], stacked[:, 2, 0]], axis=1).reshape(home_blocks, BS, -1)
    owned = jnp.take(home_kv, global_blocks % home_blocks, axis=0)
    owned = jnp.where((global_blocks // home_blocks == home_index)[:, None, None], owned, jnp.zeros_like(owned))
    global_chunk = swap_places(chunk_sum(owned, ("zh", "zl", "y")).astype(owned.dtype))
    stacked = swap_places(stacked)
    query_rows, key_rows, value_rows, grad_rows = (stacked[:, i, 0] for i in range(4))
    tokens = query_rows.shape[0]
    head_cols = query_rows.shape[1]
    heads_here = head_cols // DH
    blocks_here = tokens // BS
    lz, ly, lx = (lax.axis_size(a) for a in SEQ_AXES)
    devices = lz * ly * lx
    my_index = (lax.axis_index("x") * lz + lax.axis_index("zl")) * ly + lax.axis_index("y")
    order = [((r // ly) % lz) * (ly * lx) + (r % ly) * lx + r // (lz * ly) for r in range(devices)]
    range_at = np.argsort(np.array(order)).astype(np.int32)
    slot_of = jnp.array(order, jnp.int32)
    total_blocks = devices * blocks_here
    entries = blocks_here * NR
    capacity = (entries + devices - 1) // devices
    inv_root = 1.0 / math.sqrt(DH)
    kv_rows = jnp.concatenate([key_rows, value_rows], axis=1)
    kv_blocks = kv_rows.reshape(blocks_here, BS, 2 * head_cols)
    extended = with_halo(kv_rows, SEQ_AXES, order, BS)
    extended = extended.reshape(blocks_here + 2, BS, 2 * head_cols)
    window = jnp.stack(
        [extended[:blocks_here], extended[1 : blocks_here + 1], extended[2:]], axis=1
    )
    global_owner = global_blocks // blocks_here
    global_offset = global_blocks % blocks_here
    shared = chunk_share(global_chunk, SEQ_AXES, (devices,) + global_chunk.shape, owned.dtype)
    global_kv = jnp.take(shared, slot_of, axis=0).reshape(owned.shape)
    entry_table = random_blocks.reshape(devices, entries)
    table_owner = entry_table // blocks_here
    table_offset = entry_table % blocks_here
    positions = jnp.arange(entries, dtype=jnp.int32)
    before = positions[None, :] < positions[:, None]
    matches = (table_owner[:, :, None] == table_owner[:, None, :]) & before[None]
    table_slot = jnp.sum(matches.astype(jnp.int32), axis=2)
    my_owner = lax.dynamic_index_in_dim(table_owner, my_index, 0, keepdims=False)
    my_slot = lax.dynamic_index_in_dim(table_slot, my_index, 0, keepdims=False)
    my_target = slot_of[my_owner] * capacity + my_slot
    slot_ids = jnp.arange(capacity, dtype=jnp.int32)
    served = (table_owner == my_index)[:, :, None] & (
        table_slot[:, :, None] == slot_ids[None, None, :]
    )
    served_block = jnp.sum(jnp.where(served, table_offset[:, :, None], 0), axis=1)[range_at].reshape(-1)
    served_used = jnp.any(served, axis=1)[range_at].reshape(-1)
    outgoing = jnp.take(kv_blocks, served_block, axis=0)
    incoming = lax.all_to_all(outgoing, SEQ_AXES, split_axis=0, concat_axis=0, tiled=True)
    fetched = jnp.take(incoming, my_target, axis=0).reshape(blocks_here, NR, BS, 2 * head_cols)
    near_kv = jnp.concatenate([window, fetched], axis=1)
    near_groups = 3 + NR
    near_count = near_groups * BS
    query_heads = query_rows.reshape(blocks_here, BS, heads_here, DH)
    grad_heads = grad_rows.reshape(blocks_here, BS, heads_here, DH)
    near_keys = near_kv[..., :head_cols].reshape(blocks_here, near_groups, BS, heads_here, DH)
    near_values = near_kv[..., head_cols:].reshape(blocks_here, near_groups, BS, heads_here, DH)
    far_keys = global_kv[..., :head_cols].reshape(NG, BS, heads_here, DH)
    far_values = global_kv[..., head_cols:].reshape(NG, BS, heads_here, DH)
    scores = (
        jnp.concatenate(
            [
                jnp.einsum(
                    "bqhd,bgkhd->bhqgk", query_heads, near_keys, preferred_element_type=jnp.float32
                ).reshape(blocks_here, heads_here, BS, near_count),
                jnp.einsum(
                    "bqhd,gkhd->bhqgk", query_heads, far_keys, preferred_element_type=jnp.float32
                ).reshape(blocks_here, heads_here, BS, NG * BS),
            ],
            axis=3,
        )
        * inv_root
    )
    block_ids = my_index * blocks_here + jnp.arange(blocks_here, dtype=jnp.int32)
    usable = jnp.concatenate(
        [
            (block_ids > 0)[:, None],
            jnp.ones((blocks_here, 1), bool),
            (block_ids < total_blocks - 1)[:, None],
            jnp.ones((blocks_here, NR + NG), bool),
        ],
        axis=1,
    )
    column_ok = jnp.repeat(usable, BS, axis=1)[:, None, None, :]
    masked = jnp.where(column_ok, scores, -jnp.inf)
    row_max = jnp.max(masked, axis=3, keepdims=True)
    log_total = row_max + jnp.log(jnp.sum(jnp.exp(masked - row_max), axis=3, keepdims=True))
    probs_full = jnp.exp(masked - log_total)
    probs_half = probs_full.astype(jnp.bfloat16)
    near_probs = probs_half[..., :near_count].reshape(blocks_here, heads_here, BS, near_groups, BS)
    far_probs = probs_half[..., near_count:].reshape(blocks_here, heads_here, BS, NG, BS)
    outputs = jnp.einsum(
        "bhqgk,bgkhd->bqhd", near_probs, near_values, preferred_element_type=jnp.float32
    ) + jnp.einsum("bhqgk,gkhd->bqhd", far_probs, far_values, preferred_element_type=jnp.float32)
    row_dot = jnp.sum(grad_heads.astype(jnp.float32) * outputs, axis=3)
    dprobs = jnp.concatenate(
        [
            jnp.einsum(
                "bqhd,bgkhd->bhqgk", grad_heads, near_values, preferred_element_type=jnp.float32
            ).reshape(blocks_here, heads_here, BS, near_count),
            jnp.einsum(
                "bqhd,gkhd->bhqgk", grad_heads, far_values, preferred_element_type=jnp.float32
            ).reshape(blocks_here, heads_here, BS, NG * BS),
        ],
        axis=3,
    )
    dscores = probs_full * (dprobs - jnp.transpose(row_dot, (0, 2, 1))[..., None])
    ds_half = dscores.astype(jnp.bfloat16)
    near_ds = ds_half[..., :near_count].reshape(blocks_here, heads_here, BS, near_groups, BS)
    far_ds = ds_half[..., near_count:].reshape(blocks_here, heads_here, BS, NG, BS)
    query_grad = (
        (
            (
                jnp.einsum(
                    "bhqgk,bgkhd->bqhd", near_ds, near_keys, preferred_element_type=jnp.float32
                )
                + jnp.einsum(
                    "bhqgk,gkhd->bqhd", far_ds, far_keys, preferred_element_type=jnp.float32
                )
            )
            * inv_root
        )
        .astype(jnp.bfloat16)
        .reshape(tokens, head_cols)
    )

    def key_value_parts(ds_part, probs_part):
        key_part = (
            jnp.einsum(
                "bhqgk,bqhd->bgkhd", ds_part, query_heads, preferred_element_type=jnp.float32
            )
            * inv_root
        )
        value_part = jnp.einsum(
            "bhqgk,bqhd->bgkhd", probs_part, grad_heads, preferred_element_type=jnp.float32
        )
        out_shape = key_part.shape[:3] + (head_cols,)
        return jnp.concatenate([key_part.reshape(out_shape), value_part.reshape(out_shape)], axis=3)

    random_part = key_value_parts(near_ds[:, :, :, 3:], near_probs[:, :, :, 3:])
    random_part = random_part.astype(jnp.bfloat16).reshape(entries, BS, 2 * head_cols)
    back_rows = (
        jnp.zeros((devices * capacity, BS, 2 * head_cols), jnp.bfloat16)
        .at[my_target]
        .set(random_part)
    )
    arrived = lax.all_to_all(back_rows, SEQ_AXES, split_axis=0, concat_axis=0, tiled=True)
    window_part = key_value_parts(near_ds[:, :, :, :3], near_probs[:, :, :, :3])
    zero_block = jnp.zeros((1, BS, 2 * head_cols), jnp.float32)
    own_grad = (
        window_part[:, 1]
        + jnp.concatenate([window_part[1:, 0], zero_block], axis=0)
        + jnp.concatenate([zero_block, window_part[:-1, 2]], axis=0)
    )
    rims_out = jnp.concatenate([window_part[0, 0], window_part[blocks_here - 1, 2]], axis=0)
    rims_in = with_halo(rims_out.astype(jnp.bfloat16), SEQ_AXES, order, BS).astype(rims_out.dtype)
    own_grad = own_grad.at[0].add(rims_in[:BS]).at[blocks_here - 1].add(rims_in[3 * BS :])
    far_key = (
        jnp.einsum("bhqgk,bqhd->gkhd", far_ds, query_heads, preferred_element_type=jnp.float32)
        * inv_root
    )
    far_value = jnp.einsum(
        "bhqgk,bqhd->gkhd", far_probs, grad_heads, preferred_element_type=jnp.float32
    )
    far_part = jnp.concatenate(
        [far_key.reshape(NG, BS, head_cols), far_value.reshape(NG, BS, head_cols)], axis=2
    )
    far_sum = all_sum(far_part, SEQ_AXES)
    here_ids = jnp.arange(blocks_here, dtype=jnp.int32)
    own_global = (
        (global_owner == my_index)[None, :] & (global_offset[None, :] == here_ids[:, None])
    ).astype(jnp.float32)
    own_grad = own_grad + jnp.einsum(
        "jg,gkc->jkc", own_global, far_sum, precision=lax.Precision.HIGHEST
    )
    weights = (served_used[None, :] & (served_block[None, :] == here_ids[:, None])).astype(
        jnp.bfloat16
    )
    own_grad = own_grad + jnp.einsum(
        "jr,rkc->jkc", weights, arrived, preferred_element_type=jnp.float32
    )
    key_grad = own_grad[..., :head_cols].astype(jnp.bfloat16).reshape(tokens, head_cols)
    value_grad = own_grad[..., head_cols:].astype(jnp.bfloat16).reshape(tokens, head_cols)
    return tuple(swap_places(out) for out in (query_grad, key_grad, value_grad))


def solution(mesh):
    side = mesh.devices.shape[1] // 2
    grid = mesh.devices.reshape(-1, mesh.devices.shape[0] // (side * side), side, side, 2)
    cube = jax.sharding.Mesh(grid, ("zh", "zl", "y", "x", "core"))
    rows = ("zh", "zl", "y", "x", "core")
    placed = (P(rows, None),) * 4 + (P(), P())
    out = P(("zh", "zl", "y"), ("x", "core"))
    return jax.shard_map(
        per_device,
        mesh=cube,
        in_specs=placed,
        out_specs=(out, out, out),
        check_vma=False,
    )
```

```python
import math

import jax
import numpy as np
import jax.numpy as jnp
from jax import lax
from jax.sharding import PartitionSpec as P

DH = 128
BS = 32
NR = 3
NG = 4


def with_halo(x, axis, up, width):
    down = [(j, i) for i, j in up]
    length = x.shape[0]
    before = lax.ppermute(x[length - width :], axis, up)
    after = lax.ppermute(x[:width], axis, down)
    return jnp.concatenate([before, x, after], axis=0)


def chunk_sum(x, axis):
    peers = lax.axis_size(axis)
    parts = lax.all_to_all(x.reshape(peers, -1), axis, split_axis=0, concat_axis=0, tiled=True)
    return jnp.sum(parts.astype(jnp.float32), axis=0)


def chunk_share(chunk, axis, shape, dtype):
    peers = lax.axis_size(axis)
    copies = jnp.broadcast_to(chunk.astype(dtype)[None], (peers,) + chunk.shape)
    return lax.all_to_all(copies, axis, split_axis=0, concat_axis=0, tiled=True).reshape(shape)


def all_sum(x, axis):
    return chunk_share(chunk_sum(x, axis), axis, x.shape, x.dtype)


SEQ_AXES = ("zl", "y", "x")
SWAP_AXES = ("zh", "x")


ALL_AXES = ("zh", "zl", "y", "x", "core")


def move_slabs(x, forward):
    side = lax.axis_size("x")
    pairs = [(a * side + b, ((b - a) % side) * side + b) for a in range(side) for b in range(side)]
    if not forward:
        pairs = [(j, i) for i, j in pairs]
    return lax.ppermute(x, SWAP_AXES, pairs)


def shift_columns(x):
    side = lax.axis_size("x")
    pairs = [(a * side + b, a * side + (b - a) % side) for a in range(side) for b in range(side)]
    return lax.ppermute(x, SWAP_AXES, pairs)


def layout_tables(sizes):
    hz, lz, ly, lx, cores = sizes
    ranges = lz * ly * lx
    slot = np.zeros((hz, ranges), np.int32)
    for b in range(hz):
        for r in range(ranges):
            slot[b, r] = ((r // ly) % lz) * (ly * lx) + (r % ly) * lx + (r // (lz * ly) + b) % lx
    up = []
    for b in range(hz):
        for c in range(cores):
            for r in range(ranges - 1):
                here, there = slot[b, r], slot[b, r + 1]
                up.append(((b * ranges + here) * cores + c, (b * ranges + there) * cores + c))
    return slot, np.argsort(slot, axis=1).astype(np.int32), up


def per_device(queries, key_states, value_states, out_grad, random_blocks, global_blocks):
    groups = lax.axis_size(("x", "core"))
    rows_in, cols_in = queries.shape
    stacked = jnp.stack([queries, key_states, value_states, out_grad], axis=1)
    sizes = tuple(lax.axis_size(a) for a in ALL_AXES)
    stacked = stacked.reshape(rows_in, 4, sizes[3], groups // sizes[3], cols_in // groups)
    stacked = jnp.roll(stacked, lax.axis_index("zh"), axis=2)
    stacked = stacked.reshape(rows_in, 4, groups, cols_in // groups)
    stacked = lax.all_to_all(stacked, ("x", "core"), split_axis=2, concat_axis=0, tiled=True)
    stacked = move_slabs(stacked, True)
    query_rows, key_rows, value_rows, grad_rows = (stacked[:, i, 0] for i in range(4))
    tokens = query_rows.shape[0]
    head_cols = query_rows.shape[1]
    heads_here = head_cols // DH
    blocks_here = tokens // BS
    lz, ly, lx = (lax.axis_size(a) for a in SEQ_AXES)
    devices = lz * ly * lx
    slab = lax.axis_index("zh")
    my_index = ((lax.axis_index("x") - slab) % lx * lz + lax.axis_index("zl")) * ly + lax.axis_index("y")
    slot_table, range_table, halo_up = layout_tables(sizes)
    slot_of = jnp.asarray(slot_table)[slab]
    range_at = jnp.asarray(range_table)[slab]
    total_blocks = devices * blocks_here
    entries = blocks_here * NR
    capacity = (entries + devices - 1) // devices
    inv_root = 1.0 / math.sqrt(DH)
    kv_rows = jnp.concatenate([key_rows, value_rows], axis=1)
    kv_blocks = kv_rows.reshape(blocks_here, BS, 2 * head_cols)
    extended = with_halo(kv_rows, ALL_AXES, halo_up, BS)
    extended = extended.reshape(blocks_here + 2, BS, 2 * head_cols)
    window = jnp.stack(
        [extended[:blocks_here], extended[1 : blocks_here + 1], extended[2:]], axis=1
    )
    global_owner = global_blocks // blocks_here
    global_offset = global_blocks % blocks_here
    owned = jnp.take(kv_blocks, global_offset, axis=0)
    owned = jnp.where((global_owner == my_index)[:, None, None], owned, jnp.zeros_like(owned))
    global_kv = all_sum(owned, SEQ_AXES)
    entry_table = random_blocks.reshape(devices, entries)
    table_owner = entry_table // blocks_here
    table_offset = entry_table % blocks_here
    positions = jnp.arange(entries, dtype=jnp.int32)
    before = positions[None, :] < positions[:, None]
    matches = (table_owner[:, :, None] == table_owner[:, None, :]) & before[None]
    table_slot = jnp.sum(matches.astype(jnp.int32), axis=2)
    my_owner = lax.dynamic_index_in_dim(table_owner, my_index, 0, keepdims=False)
    my_slot = lax.dynamic_index_in_dim(table_slot, my_index, 0, keepdims=False)
    my_target = slot_of[my_owner] * capacity + my_slot
    slot_ids = jnp.arange(capacity, dtype=jnp.int32)
    served = (table_owner == my_index)[:, :, None] & (
        table_slot[:, :, None] == slot_ids[None, None, :]
    )
    served_block = jnp.sum(jnp.where(served, table_offset[:, :, None], 0), axis=1)[range_at].reshape(-1)
    served_used = jnp.any(served, axis=1)[range_at].reshape(-1)
    outgoing = jnp.take(kv_blocks, served_block, axis=0)
    incoming = lax.all_to_all(outgoing, SEQ_AXES, split_axis=0, concat_axis=0, tiled=True)
    fetched = jnp.take(incoming, my_target, axis=0).reshape(blocks_here, NR, BS, 2 * head_cols)
    near_kv = jnp.concatenate([window, fetched], axis=1)
    near_groups = 3 + NR
    near_count = near_groups * BS
    query_heads = query_rows.reshape(blocks_here, BS, heads_here, DH)
    grad_heads = grad_rows.reshape(blocks_here, BS, heads_here, DH)
    near_keys = near_kv[..., :head_cols].reshape(blocks_here, near_groups, BS, heads_here, DH)
    near_values = near_kv[..., head_cols:].reshape(blocks_here, near_groups, BS, heads_here, DH)
    far_keys = global_kv[..., :head_cols].reshape(NG, BS, heads_here, DH)
    far_values = global_kv[..., head_cols:].reshape(NG, BS, heads_here, DH)
    scores = (
        jnp.concatenate(
            [
                jnp.einsum(
                    "bqhd,bgkhd->bhqgk", query_heads, near_keys, preferred_element_type=jnp.float32
                ).reshape(blocks_here, heads_here, BS, near_count),
                jnp.einsum(
                    "bqhd,gkhd->bhqgk", query_heads, far_keys, preferred_element_type=jnp.float32
                ).reshape(blocks_here, heads_here, BS, NG * BS),
            ],
            axis=3,
        )
        * inv_root
    )
    block_ids = my_index * blocks_here + jnp.arange(blocks_here, dtype=jnp.int32)
    usable = jnp.concatenate(
        [
            (block_ids > 0)[:, None],
            jnp.ones((blocks_here, 1), bool),
            (block_ids < total_blocks - 1)[:, None],
            jnp.ones((blocks_here, NR + NG), bool),
        ],
        axis=1,
    )
    column_ok = jnp.repeat(usable, BS, axis=1)[:, None, None, :]
    masked = jnp.where(column_ok, scores, -jnp.inf)
    row_max = jnp.max(masked, axis=3, keepdims=True)
    log_total = row_max + jnp.log(jnp.sum(jnp.exp(masked - row_max), axis=3, keepdims=True))
    probs_full = jnp.exp(masked - log_total)
    probs_half = probs_full.astype(jnp.bfloat16)
    near_probs = probs_half[..., :near_count].reshape(blocks_here, heads_here, BS, near_groups, BS)
    far_probs = probs_half[..., near_count:].reshape(blocks_here, heads_here, BS, NG, BS)
    outputs = jnp.einsum(
        "bhqgk,bgkhd->bqhd", near_probs, near_values, preferred_element_type=jnp.float32
    ) + jnp.einsum("bhqgk,gkhd->bqhd", far_probs, far_values, preferred_element_type=jnp.float32)
    row_dot = jnp.sum(grad_heads.astype(jnp.float32) * outputs, axis=3)
    dprobs = jnp.concatenate(
        [
            jnp.einsum(
                "bqhd,bgkhd->bhqgk", grad_heads, near_values, preferred_element_type=jnp.float32
            ).reshape(blocks_here, heads_here, BS, near_count),
            jnp.einsum(
                "bqhd,gkhd->bhqgk", grad_heads, far_values, preferred_element_type=jnp.float32
            ).reshape(blocks_here, heads_here, BS, NG * BS),
        ],
        axis=3,
    )
    dscores = probs_full * (dprobs - jnp.transpose(row_dot, (0, 2, 1))[..., None])
    ds_half = dscores.astype(jnp.bfloat16)
    near_ds = ds_half[..., :near_count].reshape(blocks_here, heads_here, BS, near_groups, BS)
    far_ds = ds_half[..., near_count:].reshape(blocks_here, heads_here, BS, NG, BS)
    query_grad = (
        (
            (
                jnp.einsum(
                    "bhqgk,bgkhd->bqhd", near_ds, near_keys, preferred_element_type=jnp.float32
                )
                + jnp.einsum(
                    "bhqgk,gkhd->bqhd", far_ds, far_keys, preferred_element_type=jnp.float32
                )
            )
            * inv_root
        )
        .astype(jnp.bfloat16)
        .reshape(tokens, head_cols)
    )

    def key_value_parts(ds_part, probs_part):
        key_part = (
            jnp.einsum(
                "bhqgk,bqhd->bgkhd", ds_part, query_heads, preferred_element_type=jnp.float32
            )
            * inv_root
        )
        value_part = jnp.einsum(
            "bhqgk,bqhd->bgkhd", probs_part, grad_heads, preferred_element_type=jnp.float32
        )
        out_shape = key_part.shape[:3] + (head_cols,)
        return jnp.concatenate([key_part.reshape(out_shape), value_part.reshape(out_shape)], axis=3)

    random_part = key_value_parts(near_ds[:, :, :, 3:], near_probs[:, :, :, 3:])
    random_part = random_part.astype(jnp.bfloat16).reshape(entries, BS, 2 * head_cols)
    back_rows = (
        jnp.zeros((devices * capacity, BS, 2 * head_cols), jnp.bfloat16)
        .at[my_target]
        .set(random_part)
    )
    arrived = lax.all_to_all(back_rows, SEQ_AXES, split_axis=0, concat_axis=0, tiled=True)
    window_part = key_value_parts(near_ds[:, :, :, :3], near_probs[:, :, :, :3])
    zero_block = jnp.zeros((1, BS, 2 * head_cols), jnp.float32)
    own_grad = (
        window_part[:, 1]
        + jnp.concatenate([window_part[1:, 0], zero_block], axis=0)
        + jnp.concatenate([zero_block, window_part[:-1, 2]], axis=0)
    )
    rims_out = jnp.concatenate([window_part[0, 0], window_part[blocks_here - 1, 2]], axis=0)
    rims_in = with_halo(rims_out.astype(jnp.bfloat16), ALL_AXES, halo_up, BS).astype(rims_out.dtype)
    own_grad = own_grad.at[0].add(rims_in[:BS]).at[blocks_here - 1].add(rims_in[3 * BS :])
    far_key = (
        jnp.einsum("bhqgk,bqhd->gkhd", far_ds, query_heads, preferred_element_type=jnp.float32)
        * inv_root
    )
    far_value = jnp.einsum(
        "bhqgk,bqhd->gkhd", far_probs, grad_heads, preferred_element_type=jnp.float32
    )
    far_part = jnp.concatenate(
        [far_key.reshape(NG, BS, head_cols), far_value.reshape(NG, BS, head_cols)], axis=2
    )
    far_sum = all_sum(far_part, SEQ_AXES)
    here_ids = jnp.arange(blocks_here, dtype=jnp.int32)
    own_global = (
        (global_owner == my_index)[None, :] & (global_offset[None, :] == here_ids[:, None])
    ).astype(jnp.float32)
    own_grad = own_grad + jnp.einsum(
        "jg,gkc->jkc", own_global, far_sum, precision=lax.Precision.HIGHEST
    )
    weights = (served_used[None, :] & (served_block[None, :] == here_ids[:, None])).astype(
        jnp.bfloat16
    )
    own_grad = own_grad + jnp.einsum(
        "jr,rkc->jkc", weights, arrived, preferred_element_type=jnp.float32
    )
    key_grad = own_grad[..., :head_cols].astype(jnp.bfloat16).reshape(tokens, head_cols)
    value_grad = own_grad[..., head_cols:].astype(jnp.bfloat16).reshape(tokens, head_cols)
    outs = shift_columns(move_slabs(jnp.stack([query_grad, key_grad, value_grad]), False))
    return outs[0], outs[1], outs[2]


def solution(mesh):
    side = mesh.devices.shape[1] // 2
    grid = mesh.devices.reshape(-1, mesh.devices.shape[0] // (side * side), side, side, 2)
    cube = jax.sharding.Mesh(grid, ("zh", "zl", "y", "x", "core"))
    rows = ("zh", "zl", "y", "x", "core")
    placed = (P(rows, None),) * 4 + (P(), P())
    out = P(("zh", "zl", "y"), ("x", "core"))
    return jax.shard_map(
        per_device,
        mesh=cube,
        in_specs=placed,
        out_specs=(out, out, out),
        check_vma=False,
    )
```

```python
import math

import jax
import numpy as np
import jax.numpy as jnp
from jax import lax
from jax.sharding import PartitionSpec as P

DH = 128
BS = 32
NR = 3
NG = 4


def with_halo(x, axis, up, width):
    down = [(j, i) for i, j in up]
    length = x.shape[0]
    before = lax.ppermute(x[length - width :], axis, up)
    after = lax.ppermute(x[:width], axis, down)
    return jnp.concatenate([before, x, after], axis=0)


def chunk_sum(x, axis):
    peers = lax.axis_size(axis)
    parts = lax.all_to_all(x.reshape(peers, -1), axis, split_axis=0, concat_axis=0, tiled=True)
    return jnp.sum(parts.astype(jnp.float32), axis=0)


def chunk_share(chunk, axis, shape, dtype):
    peers = lax.axis_size(axis)
    copies = jnp.broadcast_to(chunk.astype(dtype)[None], (peers,) + chunk.shape)
    return lax.all_to_all(copies, axis, split_axis=0, concat_axis=0, tiled=True).reshape(shape)


def tree_sum(x, axis, index):
    peers = lax.axis_size(axis)
    bits = peers.bit_length() - 1
    parts = x.reshape(peers, -1)
    for bit in reversed(range(bits)):
        halves = parts.reshape(2, -1, parts.shape[-1])
        mine = (index >> bit) & 1
        keep = jnp.where(mine == 0, halves[0], halves[1])
        give = jnp.where(mine == 0, halves[1], halves[0])
        pairs = [(i, i ^ (1 << bit)) for i in range(peers)]
        parts = keep + lax.ppermute(give, axis, pairs)
    for bit in range(bits):
        mine = (index >> bit) & 1
        pairs = [(i, i ^ (1 << bit)) for i in range(peers)]
        other = lax.ppermute(parts, axis, pairs)
        parts = jnp.where(mine == 0, jnp.concatenate([parts, other]), jnp.concatenate([other, parts]))
    return parts.reshape(x.shape)


def all_sum(x, axis):
    return chunk_share(chunk_sum(x, axis), axis, x.shape, x.dtype)


SEQ_AXES = ("zl", "y", "x")
SWAP_AXES = ("zh", "x")


ALL_AXES = ("zh", "zl", "y", "x", "core")


def move_slabs(x, forward):
    side = lax.axis_size("x")
    pairs = [(a * side + b, ((b - a) % side) * side + b) for a in range(side) for b in range(side)]
    if not forward:
        pairs = [(j, i) for i, j in pairs]
    return lax.ppermute(x, SWAP_AXES, pairs)


def shift_columns(x):
    side = lax.axis_size("x")
    pairs = [(a * side + b, a * side + (b - a) % side) for a in range(side) for b in range(side)]
    return lax.ppermute(x, SWAP_AXES, pairs)


def layout_tables(sizes):
    hz, lz, ly, lx, cores = sizes
    ranges = lz * ly * lx
    slot = np.zeros((hz, ranges), np.int32)
    for b in range(hz):
        for r in range(ranges):
            slot[b, r] = ((r // ly) % lz) * (ly * lx) + (r % ly) * lx + (r // (lz * ly) + b) % lx
    up = []
    for b in range(hz):
        for c in range(cores):
            for r in range(ranges - 1):
                here, there = slot[b, r], slot[b, r + 1]
                up.append(((b * ranges + here) * cores + c, (b * ranges + there) * cores + c))
    return slot, np.argsort(slot, axis=1).astype(np.int32), up


def per_device(queries, key_states, value_states, out_grad, random_blocks, global_blocks):
    groups = lax.axis_size(("x", "core"))
    rows_in, cols_in = queries.shape
    stacked = jnp.stack([queries, key_states, value_states, out_grad], axis=1)
    sizes = tuple(lax.axis_size(a) for a in ALL_AXES)
    stacked = stacked.reshape(rows_in, 4, sizes[3], groups // sizes[3], cols_in // groups)
    stacked = jnp.roll(stacked, lax.axis_index("zh"), axis=2)
    stacked = stacked.reshape(rows_in, 4, groups, cols_in // groups)
    stacked = lax.all_to_all(stacked, ("x", "core"), split_axis=2, concat_axis=0, tiled=True)
    stacked = move_slabs(stacked, True)
    query_rows, key_rows, value_rows, grad_rows = (stacked[:, i, 0] for i in range(4))
    tokens = query_rows.shape[0]
    head_cols = query_rows.shape[1]
    heads_here = head_cols // DH
    blocks_here = tokens // BS
    lz, ly, lx = (lax.axis_size(a) for a in SEQ_AXES)
    devices = lz * ly * lx
    slab = lax.axis_index("zh")
    my_index = ((lax.axis_index("x") - slab) % lx * lz + lax.axis_index("zl")) * ly + lax.axis_index("y")
    slot_table, range_table, halo_up = layout_tables(sizes)
    slot_of = jnp.asarray(slot_table)[slab]
    range_at = jnp.asarray(range_table)[slab]
    total_blocks = devices * blocks_here
    entries = blocks_here * NR
    capacity = (entries + devices - 1) // devices
    inv_root = 1.0 / math.sqrt(DH)
    kv_rows = jnp.concatenate([key_rows, value_rows], axis=1)
    kv_blocks = kv_rows.reshape(blocks_here, BS, 2 * head_cols)
    extended = with_halo(kv_rows, ALL_AXES, halo_up, BS)
    extended = extended.reshape(blocks_here + 2, BS, 2 * head_cols)
    window = jnp.stack(
        [extended[:blocks_here], extended[1 : blocks_here + 1], extended[2:]], axis=1
    )
    global_owner = global_blocks // blocks_here
    global_offset = global_blocks % blocks_here
    owned = jnp.take(kv_blocks, global_offset, axis=0)
    owned = jnp.where((global_owner == my_index)[:, None, None], owned, jnp.zeros_like(owned))
    global_kv = all_sum(owned, SEQ_AXES)
    entry_table = random_blocks.reshape(devices, entries)
    table_owner = entry_table // blocks_here
    table_offset = entry_table % blocks_here
    positions = jnp.arange(entries, dtype=jnp.int32)
    before = positions[None, :] < positions[:, None]
    matches = (table_owner[:, :, None] == table_owner[:, None, :]) & before[None]
    table_slot = jnp.sum(matches.astype(jnp.int32), axis=2)
    my_owner = lax.dynamic_index_in_dim(table_owner, my_index, 0, keepdims=False)
    my_slot = lax.dynamic_index_in_dim(table_slot, my_index, 0, keepdims=False)
    my_target = slot_of[my_owner] * capacity + my_slot
    slot_ids = jnp.arange(capacity, dtype=jnp.int32)
    served = (table_owner == my_index)[:, :, None] & (
        table_slot[:, :, None] == slot_ids[None, None, :]
    )
    served_block = jnp.sum(jnp.where(served, table_offset[:, :, None], 0), axis=1)[range_at].reshape(-1)
    served_used = jnp.any(served, axis=1)[range_at].reshape(-1)
    outgoing = jnp.take(kv_blocks, served_block, axis=0)
    incoming = lax.all_to_all(outgoing, SEQ_AXES, split_axis=0, concat_axis=0, tiled=True)
    fetched = jnp.take(incoming, my_target, axis=0).reshape(blocks_here, NR, BS, 2 * head_cols)
    near_kv = jnp.concatenate([window, fetched], axis=1)
    near_groups = 3 + NR
    near_count = near_groups * BS
    query_heads = query_rows.reshape(blocks_here, BS, heads_here, DH)
    grad_heads = grad_rows.reshape(blocks_here, BS, heads_here, DH)
    near_keys = near_kv[..., :head_cols].reshape(blocks_here, near_groups, BS, heads_here, DH)
    near_values = near_kv[..., head_cols:].reshape(blocks_here, near_groups, BS, heads_here, DH)
    far_keys = global_kv[..., :head_cols].reshape(NG, BS, heads_here, DH)
    far_values = global_kv[..., head_cols:].reshape(NG, BS, heads_here, DH)
    scores = (
        jnp.concatenate(
            [
                jnp.einsum(
                    "bqhd,bgkhd->bhqgk", query_heads, near_keys, preferred_element_type=jnp.float32
                ).reshape(blocks_here, heads_here, BS, near_count),
                jnp.einsum(
                    "bqhd,gkhd->bhqgk", query_heads, far_keys, preferred_element_type=jnp.float32
                ).reshape(blocks_here, heads_here, BS, NG * BS),
            ],
            axis=3,
        )
        * inv_root
    )
    block_ids = my_index * blocks_here + jnp.arange(blocks_here, dtype=jnp.int32)
    usable = jnp.concatenate(
        [
            (block_ids > 0)[:, None],
            jnp.ones((blocks_here, 1), bool),
            (block_ids < total_blocks - 1)[:, None],
            jnp.ones((blocks_here, NR + NG), bool),
        ],
        axis=1,
    )
    column_ok = jnp.repeat(usable, BS, axis=1)[:, None, None, :]
    masked = jnp.where(column_ok, scores, -jnp.inf)
    row_max = jnp.max(masked, axis=3, keepdims=True)
    log_total = row_max + jnp.log(jnp.sum(jnp.exp(masked - row_max), axis=3, keepdims=True))
    probs_full = jnp.exp(masked - log_total)
    probs_half = probs_full.astype(jnp.bfloat16)
    near_probs = probs_half[..., :near_count].reshape(blocks_here, heads_here, BS, near_groups, BS)
    far_probs = probs_half[..., near_count:].reshape(blocks_here, heads_here, BS, NG, BS)
    outputs = jnp.einsum(
        "bhqgk,bgkhd->bqhd", near_probs, near_values, preferred_element_type=jnp.float32
    ) + jnp.einsum("bhqgk,gkhd->bqhd", far_probs, far_values, preferred_element_type=jnp.float32)
    row_dot = jnp.sum(grad_heads.astype(jnp.float32) * outputs, axis=3)
    dprobs = jnp.concatenate(
        [
            jnp.einsum(
                "bqhd,bgkhd->bhqgk", grad_heads, near_values, preferred_element_type=jnp.float32
            ).reshape(blocks_here, heads_here, BS, near_count),
            jnp.einsum(
                "bqhd,gkhd->bhqgk", grad_heads, far_values, preferred_element_type=jnp.float32
            ).reshape(blocks_here, heads_here, BS, NG * BS),
        ],
        axis=3,
    )
    dscores = probs_full * (dprobs - jnp.transpose(row_dot, (0, 2, 1))[..., None])
    ds_half = dscores.astype(jnp.bfloat16)
    near_ds = ds_half[..., :near_count].reshape(blocks_here, heads_here, BS, near_groups, BS)
    far_ds = ds_half[..., near_count:].reshape(blocks_here, heads_here, BS, NG, BS)
    query_grad = (
        (
            (
                jnp.einsum(
                    "bhqgk,bgkhd->bqhd", near_ds, near_keys, preferred_element_type=jnp.float32
                )
                + jnp.einsum(
                    "bhqgk,gkhd->bqhd", far_ds, far_keys, preferred_element_type=jnp.float32
                )
            )
            * inv_root
        )
        .astype(jnp.bfloat16)
        .reshape(tokens, head_cols)
    )

    def key_value_parts(ds_part, probs_part):
        key_part = (
            jnp.einsum(
                "bhqgk,bqhd->bgkhd", ds_part, query_heads, preferred_element_type=jnp.float32
            )
            * inv_root
        )
        value_part = jnp.einsum(
            "bhqgk,bqhd->bgkhd", probs_part, grad_heads, preferred_element_type=jnp.float32
        )
        out_shape = key_part.shape[:3] + (head_cols,)
        return jnp.concatenate([key_part.reshape(out_shape), value_part.reshape(out_shape)], axis=3)

    random_part = key_value_parts(near_ds[:, :, :, 3:], near_probs[:, :, :, 3:])
    random_part = random_part.astype(jnp.bfloat16).reshape(entries, BS, 2 * head_cols)
    back_rows = (
        jnp.zeros((devices * capacity, BS, 2 * head_cols), jnp.bfloat16)
        .at[my_target]
        .set(random_part)
    )
    arrived = lax.all_to_all(back_rows, SEQ_AXES, split_axis=0, concat_axis=0, tiled=True)
    window_part = key_value_parts(near_ds[:, :, :, :3], near_probs[:, :, :, :3])
    zero_block = jnp.zeros((1, BS, 2 * head_cols), jnp.float32)
    own_grad = (
        window_part[:, 1]
        + jnp.concatenate([window_part[1:, 0], zero_block], axis=0)
        + jnp.concatenate([zero_block, window_part[:-1, 2]], axis=0)
    )
    rims_out = jnp.concatenate([window_part[0, 0], window_part[blocks_here - 1, 2]], axis=0)
    rims_in = with_halo(rims_out.astype(jnp.bfloat16), ALL_AXES, halo_up, BS).astype(rims_out.dtype)
    own_grad = own_grad.at[0].add(rims_in[:BS]).at[blocks_here - 1].add(rims_in[3 * BS :])
    far_key = (
        jnp.einsum("bhqgk,bqhd->gkhd", far_ds, query_heads, preferred_element_type=jnp.float32)
        * inv_root
    )
    far_value = jnp.einsum(
        "bhqgk,bqhd->gkhd", far_probs, grad_heads, preferred_element_type=jnp.float32
    )
    far_part = jnp.concatenate(
        [far_key.reshape(NG, BS, head_cols), far_value.reshape(NG, BS, head_cols)], axis=2
    )
    far_sum = tree_sum(far_part, SEQ_AXES, lax.axis_index(SEQ_AXES))
    here_ids = jnp.arange(blocks_here, dtype=jnp.int32)
    own_global = (
        (global_owner == my_index)[None, :] & (global_offset[None, :] == here_ids[:, None])
    ).astype(jnp.float32)
    own_grad = own_grad + jnp.einsum(
        "jg,gkc->jkc", own_global, far_sum, precision=lax.Precision.HIGHEST
    )
    weights = (served_used[None, :] & (served_block[None, :] == here_ids[:, None])).astype(
        jnp.bfloat16
    )
    own_grad = own_grad + jnp.einsum(
        "jr,rkc->jkc", weights, arrived, preferred_element_type=jnp.float32
    )
    key_grad = own_grad[..., :head_cols].astype(jnp.bfloat16).reshape(tokens, head_cols)
    value_grad = own_grad[..., head_cols:].astype(jnp.bfloat16).reshape(tokens, head_cols)
    outs = shift_columns(move_slabs(jnp.stack([query_grad, key_grad, value_grad]), False))
    return outs[0], outs[1], outs[2]


def solution(mesh):
    side = mesh.devices.shape[1] // 2
    grid = mesh.devices.reshape(-1, mesh.devices.shape[0] // (side * side), side, side, 2)
    cube = jax.sharding.Mesh(grid, ("zh", "zl", "y", "x", "core"))
    rows = ("zh", "zl", "y", "x", "core")
    placed = (P(rows, None),) * 4 + (P(), P())
    out = P(("zh", "zl", "y"), ("x", "core"))
    return jax.shard_map(
        per_device,
        mesh=cube,
        in_specs=placed,
        out_specs=(out, out, out),
        check_vma=False,
    )
```

```python
import math

import jax
import numpy as np
import jax.numpy as jnp
from jax import lax
from jax.sharding import PartitionSpec as P

DH = 128
BS = 32
NR = 3
NG = 4


def with_halo(x, axis, up, width):
    down = [(j, i) for i, j in up]
    length = x.shape[0]
    before = lax.ppermute(x[length - width :], axis, up)
    after = lax.ppermute(x[:width], axis, down)
    return jnp.concatenate([before, x, after], axis=0)


def chunk_sum(x, axis):
    peers = lax.axis_size(axis)
    parts = lax.all_to_all(x.reshape(peers, -1), axis, split_axis=0, concat_axis=0, tiled=True)
    return jnp.sum(parts.astype(jnp.float32), axis=0)


def chunk_share(chunk, axis, shape, dtype):
    peers = lax.axis_size(axis)
    copies = jnp.broadcast_to(chunk.astype(dtype)[None], (peers,) + chunk.shape)
    return lax.all_to_all(copies, axis, split_axis=0, concat_axis=0, tiled=True).reshape(shape)


def carry_along(slots, extra, peers, capacity):
    rows, lanes = slots.shape[1], slots.shape[2]
    slot_rows = capacity * rows
    width = extra.shape[1]
    wide = -(-width // (slot_rows * 128)) * 128
    pad = jnp.zeros((peers, slot_rows * wide - width), extra.dtype)
    extra = jnp.concatenate([extra, pad], axis=1).reshape(peers, slot_rows, wide)
    both = jnp.concatenate([slots.reshape(peers, slot_rows, lanes), extra], axis=2)
    both = lax.all_to_all(both, SEQ_AXES, split_axis=0, concat_axis=0, tiled=True)
    main = both[..., :lanes].reshape(slots.shape)
    return main, both[..., lanes:].reshape(peers, -1)[:, :width]


def far_gradient(far_ds, far_probs, query_heads, grad_heads, head_cols):
    inv_root = 1.0 / math.sqrt(DH)
    far_key = (
        jnp.einsum("bhqgk,bqhd->gkhd", far_ds, query_heads, preferred_element_type=jnp.float32)
        * inv_root
    )
    far_value = jnp.einsum(
        "bhqgk,bqhd->gkhd", far_probs, grad_heads, preferred_element_type=jnp.float32
    )
    return jnp.concatenate(
        [far_key.reshape(NG, BS, head_cols), far_value.reshape(NG, BS, head_cols)], axis=2
    )


def all_sum(x, axis):
    return chunk_share(chunk_sum(x, axis), axis, x.shape, x.dtype)


SEQ_AXES = ("zl", "y", "x")
SWAP_AXES = ("zh", "x")


ALL_AXES = ("zh", "zl", "y", "x", "core")


def move_slabs(x, forward):
    side = lax.axis_size("x")
    pairs = [(a * side + b, ((b - a) % side) * side + b) for a in range(side) for b in range(side)]
    if not forward:
        pairs = [(j, i) for i, j in pairs]
    return lax.ppermute(x, SWAP_AXES, pairs)


def shift_columns(x):
    side = lax.axis_size("x")
    pairs = [(a * side + b, a * side + (b - a) % side) for a in range(side) for b in range(side)]
    return lax.ppermute(x, SWAP_AXES, pairs)


def layout_tables(sizes):
    hz, lz, ly, lx, cores = sizes
    ranges = lz * ly * lx
    slot = np.zeros((hz, ranges), np.int32)
    for b in range(hz):
        for r in range(ranges):
            slot[b, r] = ((r // ly) % lz) * (ly * lx) + (r % ly) * lx + (r // (lz * ly) + b) % lx
    up = []
    for b in range(hz):
        for c in range(cores):
            for r in range(ranges - 1):
                here, there = slot[b, r], slot[b, r + 1]
                up.append(((b * ranges + here) * cores + c, (b * ranges + there) * cores + c))
    return slot, np.argsort(slot, axis=1).astype(np.int32), up


def per_device(queries, key_states, value_states, out_grad, random_blocks, global_blocks):
    groups = lax.axis_size(("x", "core"))
    rows_in, cols_in = queries.shape
    stacked = jnp.stack([queries, key_states, value_states, out_grad], axis=1)
    sizes = tuple(lax.axis_size(a) for a in ALL_AXES)
    stacked = stacked.reshape(rows_in, 4, sizes[3], groups // sizes[3], cols_in // groups)
    stacked = jnp.roll(stacked, lax.axis_index("zh"), axis=2)
    stacked = stacked.reshape(rows_in, 4, groups, cols_in // groups)
    stacked = lax.all_to_all(stacked, ("x", "core"), split_axis=2, concat_axis=0, tiled=True)
    stacked = move_slabs(stacked, True)
    query_rows, key_rows, value_rows, grad_rows = (stacked[:, i, 0] for i in range(4))
    tokens = query_rows.shape[0]
    head_cols = query_rows.shape[1]
    heads_here = head_cols // DH
    blocks_here = tokens // BS
    lz, ly, lx = (lax.axis_size(a) for a in SEQ_AXES)
    devices = lz * ly * lx
    slab = lax.axis_index("zh")
    my_index = ((lax.axis_index("x") - slab) % lx * lz + lax.axis_index("zl")) * ly + lax.axis_index("y")
    slot_table, range_table, halo_up = layout_tables(sizes)
    slot_of = jnp.asarray(slot_table)[slab]
    range_at = jnp.asarray(range_table)[slab]
    total_blocks = devices * blocks_here
    entries = blocks_here * NR
    capacity = (entries + devices - 1) // devices
    inv_root = 1.0 / math.sqrt(DH)
    kv_rows = jnp.concatenate([key_rows, value_rows], axis=1)
    kv_blocks = kv_rows.reshape(blocks_here, BS, 2 * head_cols)
    extended = with_halo(kv_rows, ALL_AXES, halo_up, BS)
    extended = extended.reshape(blocks_here + 2, BS, 2 * head_cols)
    window = jnp.stack(
        [extended[:blocks_here], extended[1 : blocks_here + 1], extended[2:]], axis=1
    )
    global_owner = global_blocks // blocks_here
    global_offset = global_blocks % blocks_here
    owned = jnp.take(kv_blocks, global_offset, axis=0)
    owned = jnp.where((global_owner == my_index)[:, None, None], owned, jnp.zeros_like(owned))
    entry_table = random_blocks.reshape(devices, entries)
    table_owner = entry_table // blocks_here
    table_offset = entry_table % blocks_here
    positions = jnp.arange(entries, dtype=jnp.int32)
    before = positions[None, :] < positions[:, None]
    matches = (table_owner[:, :, None] == table_owner[:, None, :]) & before[None]
    table_slot = jnp.sum(matches.astype(jnp.int32), axis=2)
    my_owner = lax.dynamic_index_in_dim(table_owner, my_index, 0, keepdims=False)
    my_slot = lax.dynamic_index_in_dim(table_slot, my_index, 0, keepdims=False)
    my_target = slot_of[my_owner] * capacity + my_slot
    slot_ids = jnp.arange(capacity, dtype=jnp.int32)
    served = (table_owner == my_index)[:, :, None] & (
        table_slot[:, :, None] == slot_ids[None, None, :]
    )
    served_block = jnp.sum(jnp.where(served, table_offset[:, :, None], 0), axis=1)[range_at].reshape(-1)
    served_used = jnp.any(served, axis=1)[range_at].reshape(-1)
    outgoing = jnp.take(kv_blocks, served_block, axis=0)
    incoming, global_parts = carry_along(outgoing, owned.reshape(devices, -1), devices, capacity)
    global_chunk = jnp.sum(global_parts.astype(jnp.float32), axis=0)
    global_kv = chunk_share(global_chunk, SEQ_AXES, owned.shape, owned.dtype)
    fetched = jnp.take(incoming, my_target, axis=0).reshape(blocks_here, NR, BS, 2 * head_cols)
    near_kv = jnp.concatenate([window, fetched], axis=1)
    near_groups = 3 + NR
    near_count = near_groups * BS
    query_heads = query_rows.reshape(blocks_here, BS, heads_here, DH)
    grad_heads = grad_rows.reshape(blocks_here, BS, heads_here, DH)
    near_keys = near_kv[..., :head_cols].reshape(blocks_here, near_groups, BS, heads_here, DH)
    near_values = near_kv[..., head_cols:].reshape(blocks_here, near_groups, BS, heads_here, DH)
    far_keys = global_kv[..., :head_cols].reshape(NG, BS, heads_here, DH)
    far_values = global_kv[..., head_cols:].reshape(NG, BS, heads_here, DH)
    scores = (
        jnp.concatenate(
            [
                jnp.einsum(
                    "bqhd,bgkhd->bhqgk", query_heads, near_keys, preferred_element_type=jnp.float32
                ).reshape(blocks_here, heads_here, BS, near_count),
                jnp.einsum(
                    "bqhd,gkhd->bhqgk", query_heads, far_keys, preferred_element_type=jnp.float32
                ).reshape(blocks_here, heads_here, BS, NG * BS),
            ],
            axis=3,
        )
        * inv_root
    )
    block_ids = my_index * blocks_here + jnp.arange(blocks_here, dtype=jnp.int32)
    usable = jnp.concatenate(
        [
            (block_ids > 0)[:, None],
            jnp.ones((blocks_here, 1), bool),
            (block_ids < total_blocks - 1)[:, None],
            jnp.ones((blocks_here, NR + NG), bool),
        ],
        axis=1,
    )
    column_ok = jnp.repeat(usable, BS, axis=1)[:, None, None, :]
    masked = jnp.where(column_ok, scores, -jnp.inf)
    row_max = jnp.max(masked, axis=3, keepdims=True)
    log_total = row_max + jnp.log(jnp.sum(jnp.exp(masked - row_max), axis=3, keepdims=True))
    probs_full = jnp.exp(masked - log_total)
    probs_half = probs_full.astype(jnp.bfloat16)
    near_probs = probs_half[..., :near_count].reshape(blocks_here, heads_here, BS, near_groups, BS)
    far_probs = probs_half[..., near_count:].reshape(blocks_here, heads_here, BS, NG, BS)
    outputs = jnp.einsum(
        "bhqgk,bgkhd->bqhd", near_probs, near_values, preferred_element_type=jnp.float32
    ) + jnp.einsum("bhqgk,gkhd->bqhd", far_probs, far_values, preferred_element_type=jnp.float32)
    row_dot = jnp.sum(grad_heads.astype(jnp.float32) * outputs, axis=3)
    dprobs = jnp.concatenate(
        [
            jnp.einsum(
                "bqhd,bgkhd->bhqgk", grad_heads, near_values, preferred_element_type=jnp.float32
            ).reshape(blocks_here, heads_here, BS, near_count),
            jnp.einsum(
                "bqhd,gkhd->bhqgk", grad_heads, far_values, preferred_element_type=jnp.float32
            ).reshape(blocks_here, heads_here, BS, NG * BS),
        ],
        axis=3,
    )
    dscores = probs_full * (dprobs - jnp.transpose(row_dot, (0, 2, 1))[..., None])
    ds_half = dscores.astype(jnp.bfloat16)
    near_ds = ds_half[..., :near_count].reshape(blocks_here, heads_here, BS, near_groups, BS)
    far_ds = ds_half[..., near_count:].reshape(blocks_here, heads_here, BS, NG, BS)
    query_grad = (
        (
            (
                jnp.einsum(
                    "bhqgk,bgkhd->bqhd", near_ds, near_keys, preferred_element_type=jnp.float32
                )
                + jnp.einsum(
                    "bhqgk,gkhd->bqhd", far_ds, far_keys, preferred_element_type=jnp.float32
                )
            )
            * inv_root
        )
        .astype(jnp.bfloat16)
        .reshape(tokens, head_cols)
    )

    def key_value_parts(ds_part, probs_part):
        key_part = (
            jnp.einsum(
                "bhqgk,bqhd->bgkhd", ds_part, query_heads, preferred_element_type=jnp.float32
            )
            * inv_root
        )
        value_part = jnp.einsum(
            "bhqgk,bqhd->bgkhd", probs_part, grad_heads, preferred_element_type=jnp.float32
        )
        out_shape = key_part.shape[:3] + (head_cols,)
        return jnp.concatenate([key_part.reshape(out_shape), value_part.reshape(out_shape)], axis=3)

    random_part = key_value_parts(near_ds[:, :, :, 3:], near_probs[:, :, :, 3:])
    random_part = random_part.astype(jnp.bfloat16).reshape(entries, BS, 2 * head_cols)
    back_rows = (
        jnp.zeros((devices * capacity, BS, 2 * head_cols), jnp.bfloat16)
        .at[my_target]
        .set(random_part)
    )
    far_part = far_gradient(far_ds, far_probs, query_heads, grad_heads, head_cols)
    far_flat = far_part.reshape(devices, -1)
    far_high = far_flat.astype(jnp.bfloat16)
    far_low = (far_flat - far_high.astype(jnp.float32)).astype(jnp.bfloat16)
    arrived, far_parts = carry_along(
        back_rows, jnp.concatenate([far_high, far_low], axis=1), devices, capacity
    )
    half = far_flat.shape[1]
    far_chunk = jnp.sum(
        far_parts[:, :half].astype(jnp.float32) + far_parts[:, half:].astype(jnp.float32), axis=0
    )
    far_sum = chunk_share(far_chunk, SEQ_AXES, far_part.shape, far_part.dtype)
    window_part = key_value_parts(near_ds[:, :, :, :3], near_probs[:, :, :, :3])
    zero_block = jnp.zeros((1, BS, 2 * head_cols), jnp.float32)
    own_grad = (
        window_part[:, 1]
        + jnp.concatenate([window_part[1:, 0], zero_block], axis=0)
        + jnp.concatenate([zero_block, window_part[:-1, 2]], axis=0)
    )
    rims_out = jnp.concatenate([window_part[0, 0], window_part[blocks_here - 1, 2]], axis=0)
    rims_in = with_halo(rims_out.astype(jnp.bfloat16), ALL_AXES, halo_up, BS).astype(rims_out.dtype)
    own_grad = own_grad.at[0].add(rims_in[:BS]).at[blocks_here - 1].add(rims_in[3 * BS :])
    here_ids = jnp.arange(blocks_here, dtype=jnp.int32)
    own_global = (
        (global_owner == my_index)[None, :] & (global_offset[None, :] == here_ids[:, None])
    ).astype(jnp.float32)
    own_grad = own_grad + jnp.einsum(
        "jg,gkc->jkc", own_global, far_sum, precision=lax.Precision.HIGHEST
    )
    weights = (served_used[None, :] & (served_block[None, :] == here_ids[:, None])).astype(
        jnp.bfloat16
    )
    own_grad = own_grad + jnp.einsum(
        "jr,rkc->jkc", weights, arrived, preferred_element_type=jnp.float32
    )
    key_grad = own_grad[..., :head_cols].astype(jnp.bfloat16).reshape(tokens, head_cols)
    value_grad = own_grad[..., head_cols:].astype(jnp.bfloat16).reshape(tokens, head_cols)
    outs = shift_columns(move_slabs(jnp.stack([query_grad, key_grad, value_grad]), False))
    return outs[0], outs[1], outs[2]


def solution(mesh):
    side = mesh.devices.shape[1] // 2
    grid = mesh.devices.reshape(-1, mesh.devices.shape[0] // (side * side), side, side, 2)
    cube = jax.sharding.Mesh(grid, ("zh", "zl", "y", "x", "core"))
    rows = ("zh", "zl", "y", "x", "core")
    placed = (P(rows, None),) * 4 + (P(), P())
    out = P(("zh", "zl", "y"), ("x", "core"))
    return jax.shard_map(
        per_device,
        mesh=cube,
        in_specs=placed,
        out_specs=(out, out, out),
        check_vma=False,
    )
```

```python
import math

import jax
import numpy as np
import jax.numpy as jnp
from jax import lax
from jax.sharding import PartitionSpec as P

DH = 128
BS = 32
NR = 3
NG = 4


def with_halo(x, axis, up, width):
    down = [(j, i) for i, j in up]
    length = x.shape[0]
    before = lax.ppermute(x[length - width :], axis, up)
    after = lax.ppermute(x[:width], axis, down)
    return jnp.concatenate([before, x, after], axis=0)


def chunk_sum(x, axis):
    peers = lax.axis_size(axis)
    parts = lax.all_to_all(x.reshape(peers, -1), axis, split_axis=0, concat_axis=0, tiled=True)
    return jnp.sum(parts.astype(jnp.float32), axis=0)


def chunk_share(chunk, axis, shape, dtype):
    peers = lax.axis_size(axis)
    copies = jnp.broadcast_to(chunk.astype(dtype)[None], (peers,) + chunk.shape)
    return lax.all_to_all(copies, axis, split_axis=0, concat_axis=0, tiled=True).reshape(shape)


def all_sum(x, axis):
    return chunk_share(chunk_sum(x, axis), axis, x.shape, x.dtype)


SEQ_AXES = ("zl", "y", "x")
SWAP_AXES = ("zh", "x")


ALL_AXES = ("zh", "zl", "y", "x", "core")


def move_slabs(x, forward):
    side = lax.axis_size("x")
    pairs = [(a * side + b, ((b - a) % side) * side + b) for a in range(side) for b in range(side)]
    if not forward:
        pairs = [(j, i) for i, j in pairs]
    return lax.ppermute(x, SWAP_AXES, pairs)


def shift_columns(x):
    side = lax.axis_size("x")
    pairs = [(a * side + b, a * side + (b - a) % side) for a in range(side) for b in range(side)]
    return lax.ppermute(x, SWAP_AXES, pairs)


def layout_tables(sizes):
    hz, lz, ly, lx, cores = sizes
    ranges = lz * ly * lx
    slot = np.zeros((hz, ranges), np.int32)
    for b in range(hz):
        for r in range(ranges):
            slot[b, r] = ((r // ly) % lz) * (ly * lx) + (r % ly) * lx + (r // (lz * ly) + b) % lx
    up = []
    for b in range(hz):
        for c in range(cores):
            for r in range(ranges - 1):
                here, there = slot[b, r], slot[b, r + 1]
                up.append(((b * ranges + here) * cores + c, (b * ranges + there) * cores + c))
    return slot, np.argsort(slot, axis=1).astype(np.int32), up


def per_device(queries, key_states, value_states, out_grad, random_blocks, global_blocks):
    groups = lax.axis_size(("x", "core"))
    rows_in, cols_in = queries.shape
    sizes = tuple(lax.axis_size(a) for a in ALL_AXES)

    def bring(pair):
        stacked = jnp.stack(pair, axis=1)
        stacked = stacked.reshape(rows_in, 2, sizes[3], groups // sizes[3], cols_in // groups)
        stacked = jnp.roll(stacked, lax.axis_index("zh"), axis=2)
        stacked = stacked.reshape(rows_in, 2, groups, cols_in // groups)
        stacked = lax.all_to_all(stacked, ("x", "core"), split_axis=2, concat_axis=0, tiled=True)
        stacked = move_slabs(stacked, True)
        return stacked[:, 0, 0], stacked[:, 1, 0]

    key_rows, value_rows = bring([key_states, value_states])
    query_rows, grad_rows = bring([queries, out_grad])
    tokens = query_rows.shape[0]
    head_cols = query_rows.shape[1]
    heads_here = head_cols // DH
    blocks_here = tokens // BS
    lz, ly, lx = (lax.axis_size(a) for a in SEQ_AXES)
    devices = lz * ly * lx
    slab = lax.axis_index("zh")
    my_index = ((lax.axis_index("x") - slab) % lx * lz + lax.axis_index("zl")) * ly + lax.axis_index("y")
    slot_table, range_table, halo_up = layout_tables(sizes)
    slot_of = jnp.asarray(slot_table)[slab]
    range_at = jnp.asarray(range_table)[slab]
    total_blocks = devices * blocks_here
    entries = blocks_here * NR
    capacity = (entries + devices - 1) // devices
    inv_root = 1.0 / math.sqrt(DH)
    kv_rows = jnp.concatenate([key_rows, value_rows], axis=1)
    kv_blocks = kv_rows.reshape(blocks_here, BS, 2 * head_cols)
    extended = with_halo(kv_rows, ALL_AXES, halo_up, BS)
    extended = extended.reshape(blocks_here + 2, BS, 2 * head_cols)
    window = jnp.stack(
        [extended[:blocks_here], extended[1 : blocks_here + 1], extended[2:]], axis=1
    )
    global_owner = global_blocks // blocks_here
    global_offset = global_blocks % blocks_here
    owned = jnp.take(kv_blocks, global_offset, axis=0)
    owned = jnp.where((global_owner == my_index)[:, None, None], owned, jnp.zeros_like(owned))
    global_kv = all_sum(owned, SEQ_AXES)
    entry_table = random_blocks.reshape(devices, entries)
    table_owner = entry_table // blocks_here
    table_offset = entry_table % blocks_here
    positions = jnp.arange(entries, dtype=jnp.int32)
    before = positions[None, :] < positions[:, None]
    matches = (table_owner[:, :, None] == table_owner[:, None, :]) & before[None]
    table_slot = jnp.sum(matches.astype(jnp.int32), axis=2)
    my_owner = lax.dynamic_index_in_dim(table_owner, my_index, 0, keepdims=False)
    my_slot = lax.dynamic_index_in_dim(table_slot, my_index, 0, keepdims=False)
    my_target = slot_of[my_owner] * capacity + my_slot
    slot_ids = jnp.arange(capacity, dtype=jnp.int32)
    served = (table_owner == my_index)[:, :, None] & (
        table_slot[:, :, None] == slot_ids[None, None, :]
    )
    served_block = jnp.sum(jnp.where(served, table_offset[:, :, None], 0), axis=1)[range_at].reshape(-1)
    served_used = jnp.any(served, axis=1)[range_at].reshape(-1)
    outgoing = jnp.take(kv_blocks, served_block, axis=0)
    incoming = lax.all_to_all(outgoing, SEQ_AXES, split_axis=0, concat_axis=0, tiled=True)
    fetched = jnp.take(incoming, my_target, axis=0).reshape(blocks_here, NR, BS, 2 * head_cols)
    near_kv = jnp.concatenate([window, fetched], axis=1)
    near_groups = 3 + NR
    near_count = near_groups * BS
    query_heads = query_rows.reshape(blocks_here, BS, heads_here, DH)
    grad_heads = grad_rows.reshape(blocks_here, BS, heads_here, DH)
    near_keys = near_kv[..., :head_cols].reshape(blocks_here, near_groups, BS, heads_here, DH)
    near_values = near_kv[..., head_cols:].reshape(blocks_here, near_groups, BS, heads_here, DH)
    far_keys = global_kv[..., :head_cols].reshape(NG, BS, heads_here, DH)
    far_values = global_kv[..., head_cols:].reshape(NG, BS, heads_here, DH)
    scores = (
        jnp.concatenate(
            [
                jnp.einsum(
                    "bqhd,bgkhd->bhqgk", query_heads, near_keys, preferred_element_type=jnp.float32
                ).reshape(blocks_here, heads_here, BS, near_count),
                jnp.einsum(
                    "bqhd,gkhd->bhqgk", query_heads, far_keys, preferred_element_type=jnp.float32
                ).reshape(blocks_here, heads_here, BS, NG * BS),
            ],
            axis=3,
        )
        * inv_root
    )
    block_ids = my_index * blocks_here + jnp.arange(blocks_here, dtype=jnp.int32)
    usable = jnp.concatenate(
        [
            (block_ids > 0)[:, None],
            jnp.ones((blocks_here, 1), bool),
            (block_ids < total_blocks - 1)[:, None],
            jnp.ones((blocks_here, NR + NG), bool),
        ],
        axis=1,
    )
    column_ok = jnp.repeat(usable, BS, axis=1)[:, None, None, :]
    masked = jnp.where(column_ok, scores, -jnp.inf)
    row_max = jnp.max(masked, axis=3, keepdims=True)
    log_total = row_max + jnp.log(jnp.sum(jnp.exp(masked - row_max), axis=3, keepdims=True))
    probs_full = jnp.exp(masked - log_total)
    probs_half = probs_full.astype(jnp.bfloat16)
    near_probs = probs_half[..., :near_count].reshape(blocks_here, heads_here, BS, near_groups, BS)
    far_probs = probs_half[..., near_count:].reshape(blocks_here, heads_here, BS, NG, BS)
    outputs = jnp.einsum(
        "bhqgk,bgkhd->bqhd", near_probs, near_values, preferred_element_type=jnp.float32
    ) + jnp.einsum("bhqgk,gkhd->bqhd", far_probs, far_values, preferred_element_type=jnp.float32)
    row_dot = jnp.sum(grad_heads.astype(jnp.float32) * outputs, axis=3)
    dprobs = jnp.concatenate(
        [
            jnp.einsum(
                "bqhd,bgkhd->bhqgk", grad_heads, near_values, preferred_element_type=jnp.float32
            ).reshape(blocks_here, heads_here, BS, near_count),
            jnp.einsum(
                "bqhd,gkhd->bhqgk", grad_heads, far_values, preferred_element_type=jnp.float32
            ).reshape(blocks_here, heads_here, BS, NG * BS),
        ],
        axis=3,
    )
    dscores = probs_full * (dprobs - jnp.transpose(row_dot, (0, 2, 1))[..., None])
    ds_half = dscores.astype(jnp.bfloat16)
    near_ds = ds_half[..., :near_count].reshape(blocks_here, heads_here, BS, near_groups, BS)
    far_ds = ds_half[..., near_count:].reshape(blocks_here, heads_here, BS, NG, BS)
    query_grad = (
        (
            (
                jnp.einsum(
                    "bhqgk,bgkhd->bqhd", near_ds, near_keys, preferred_element_type=jnp.float32
                )
                + jnp.einsum(
                    "bhqgk,gkhd->bqhd", far_ds, far_keys, preferred_element_type=jnp.float32
                )
            )
            * inv_root
        )
        .astype(jnp.bfloat16)
        .reshape(tokens, head_cols)
    )

    def key_value_parts(ds_part, probs_part):
        key_part = (
            jnp.einsum(
                "bhqgk,bqhd->bgkhd", ds_part, query_heads, preferred_element_type=jnp.float32
            )
            * inv_root
        )
        value_part = jnp.einsum(
            "bhqgk,bqhd->bgkhd", probs_part, grad_heads, preferred_element_type=jnp.float32
        )
        out_shape = key_part.shape[:3] + (head_cols,)
        return jnp.concatenate([key_part.reshape(out_shape), value_part.reshape(out_shape)], axis=3)

    random_part = key_value_parts(near_ds[:, :, :, 3:], near_probs[:, :, :, 3:])
    random_part = random_part.astype(jnp.bfloat16).reshape(entries, BS, 2 * head_cols)
    back_rows = (
        jnp.zeros((devices * capacity, BS, 2 * head_cols), jnp.bfloat16)
        .at[my_target]
        .set(random_part)
    )
    arrived = lax.all_to_all(back_rows, SEQ_AXES, split_axis=0, concat_axis=0, tiled=True)
    window_part = key_value_parts(near_ds[:, :, :, :3], near_probs[:, :, :, :3])
    zero_block = jnp.zeros((1, BS, 2 * head_cols), jnp.float32)
    own_grad = (
        window_part[:, 1]
        + jnp.concatenate([window_part[1:, 0], zero_block], axis=0)
        + jnp.concatenate([zero_block, window_part[:-1, 2]], axis=0)
    )
    rims_out = jnp.concatenate([window_part[0, 0], window_part[blocks_here - 1, 2]], axis=0)
    rims_in = with_halo(rims_out.astype(jnp.bfloat16), ALL_AXES, halo_up, BS).astype(rims_out.dtype)
    own_grad = own_grad.at[0].add(rims_in[:BS]).at[blocks_here - 1].add(rims_in[3 * BS :])
    far_key = (
        jnp.einsum("bhqgk,bqhd->gkhd", far_ds, query_heads, preferred_element_type=jnp.float32)
        * inv_root
    )
    far_value = jnp.einsum(
        "bhqgk,bqhd->gkhd", far_probs, grad_heads, preferred_element_type=jnp.float32
    )
    far_part = jnp.concatenate(
        [far_key.reshape(NG, BS, head_cols), far_value.reshape(NG, BS, head_cols)], axis=2
    )
    far_sum = all_sum(far_part, SEQ_AXES)
    here_ids = jnp.arange(blocks_here, dtype=jnp.int32)
    own_global = (
        (global_owner == my_index)[None, :] & (global_offset[None, :] == here_ids[:, None])
    ).astype(jnp.float32)
    own_grad = own_grad + jnp.einsum(
        "jg,gkc->jkc", own_global, far_sum, precision=lax.Precision.HIGHEST
    )
    weights = (served_used[None, :] & (served_block[None, :] == here_ids[:, None])).astype(
        jnp.bfloat16
    )
    own_grad = own_grad + jnp.einsum(
        "jr,rkc->jkc", weights, arrived, preferred_element_type=jnp.float32
    )
    key_grad = own_grad[..., :head_cols].astype(jnp.bfloat16).reshape(tokens, head_cols)
    value_grad = own_grad[..., head_cols:].astype(jnp.bfloat16).reshape(tokens, head_cols)
    outs = shift_columns(move_slabs(jnp.stack([query_grad, key_grad, value_grad]), False))
    return outs[0], outs[1], outs[2]


def solution(mesh):
    side = mesh.devices.shape[1] // 2
    grid = mesh.devices.reshape(-1, mesh.devices.shape[0] // (side * side), side, side, 2)
    cube = jax.sharding.Mesh(grid, ("zh", "zl", "y", "x", "core"))
    rows = ("zh", "zl", "y", "x", "core")
    placed = (P(rows, None),) * 4 + (P(), P())
    out = P(("zh", "zl", "y"), ("x", "core"))
    return jax.shard_map(
        per_device,
        mesh=cube,
        in_specs=placed,
        out_specs=(out, out, out),
        check_vma=False,
    )
```

```python
import math

import jax
import numpy as np
import jax.numpy as jnp
from jax import lax
from jax.sharding import PartitionSpec as P

DH = 128
BS = 32
NR = 3
NG = 4


def with_halo(x, axis, up, width):
    down = [(j, i) for i, j in up]
    length = x.shape[0]
    before = lax.ppermute(x[length - width :], axis, up)
    after = lax.ppermute(x[:width], axis, down)
    return jnp.concatenate([before, x, after], axis=0)


def chunk_sum(x, axis):
    peers = lax.axis_size(axis)
    parts = lax.all_to_all(x.reshape(peers, -1), axis, split_axis=0, concat_axis=0, tiled=True)
    return jnp.sum(parts.astype(jnp.float32), axis=0)


def chunk_share(chunk, axis, shape, dtype):
    peers = lax.axis_size(axis)
    copies = jnp.broadcast_to(chunk.astype(dtype)[None], (peers,) + chunk.shape)
    return lax.all_to_all(copies, axis, split_axis=0, concat_axis=0, tiled=True).reshape(shape)


def all_sum(x, axis):
    return chunk_share(chunk_sum(x, axis), axis, x.shape, x.dtype)


SEQ_AXES = ("zl", "y", "x")
SWAP_AXES = ("zh", "x")


ALL_AXES = ("zh", "zl", "y", "x", "core")


def move_slabs(x, forward):
    side = lax.axis_size("x")
    pairs = [(a * side + b, ((b - a) % side) * side + b) for a in range(side) for b in range(side)]
    if not forward:
        pairs = [(j, i) for i, j in pairs]
    return lax.ppermute(x, SWAP_AXES, pairs)


def shift_columns(x):
    side = lax.axis_size("x")
    pairs = [(a * side + b, a * side + (b - a) % side) for a in range(side) for b in range(side)]
    return lax.ppermute(x, SWAP_AXES, pairs)


def send_home(x):
    side = lax.axis_size("x")
    pairs = [(b * side + x, ((x - b) % side) * side + b) for b in range(side) for x in range(side)]
    return lax.ppermute(x, SWAP_AXES, pairs)


def layout_tables(sizes):
    hz, lz, ly, lx, cores = sizes
    ranges = lz * ly * lx
    slot = np.zeros((hz, ranges), np.int32)
    for b in range(hz):
        for r in range(ranges):
            slot[b, r] = ((r // ly) % lz) * (ly * lx) + (r % ly) * lx + (r // (lz * ly) + b) % lx
    up = []
    for b in range(hz):
        for c in range(cores):
            for r in range(ranges - 1):
                here, there = slot[b, r], slot[b, r + 1]
                up.append(((b * ranges + here) * cores + c, (b * ranges + there) * cores + c))
    return slot, np.argsort(slot, axis=1).astype(np.int32), up


def per_device(queries, key_states, value_states, out_grad, random_blocks, global_blocks):
    groups = lax.axis_size(("x", "core"))
    rows_in, cols_in = queries.shape
    stacked = jnp.stack([queries, key_states, value_states, out_grad], axis=1)
    sizes = tuple(lax.axis_size(a) for a in ALL_AXES)
    stacked = stacked.reshape(rows_in, 4, sizes[3], groups // sizes[3], cols_in // groups)
    stacked = jnp.roll(stacked, lax.axis_index("zh"), axis=2)
    stacked = stacked.reshape(rows_in, 4, groups, cols_in // groups)
    stacked = lax.all_to_all(stacked, ("x", "core"), split_axis=2, concat_axis=0, tiled=True)
    stacked = move_slabs(stacked, True)
    query_rows, key_rows, value_rows, grad_rows = (stacked[:, i, 0] for i in range(4))
    tokens = query_rows.shape[0]
    head_cols = query_rows.shape[1]
    heads_here = head_cols // DH
    blocks_here = tokens // BS
    lz, ly, lx = (lax.axis_size(a) for a in SEQ_AXES)
    devices = lz * ly * lx
    slab = lax.axis_index("zh")
    my_index = ((lax.axis_index("x") - slab) % lx * lz + lax.axis_index("zl")) * ly + lax.axis_index("y")
    slot_table, range_table, halo_up = layout_tables(sizes)
    slot_of = jnp.asarray(slot_table)[slab]
    range_at = jnp.asarray(range_table)[slab]
    total_blocks = devices * blocks_here
    entries = blocks_here * NR
    capacity = (entries + devices - 1) // devices
    inv_root = 1.0 / math.sqrt(DH)
    kv_rows = jnp.concatenate([key_rows, value_rows], axis=1)
    kv_blocks = kv_rows.reshape(blocks_here, BS, 2 * head_cols)
    extended = with_halo(kv_rows, ALL_AXES, halo_up, BS)
    extended = extended.reshape(blocks_here + 2, BS, 2 * head_cols)
    window = jnp.stack(
        [extended[:blocks_here], extended[1 : blocks_here + 1], extended[2:]], axis=1
    )
    global_owner = global_blocks // blocks_here
    global_offset = global_blocks % blocks_here
    owned = jnp.take(kv_blocks, global_offset, axis=0)
    owned = jnp.where((global_owner == my_index)[:, None, None], owned, jnp.zeros_like(owned))
    global_kv = all_sum(owned, SEQ_AXES)
    entry_table = random_blocks.reshape(devices, entries)
    table_owner = entry_table // blocks_here
    table_offset = entry_table % blocks_here
    positions = jnp.arange(entries, dtype=jnp.int32)
    before = positions[None, :] < positions[:, None]
    matches = (table_owner[:, :, None] == table_owner[:, None, :]) & before[None]
    table_slot = jnp.sum(matches.astype(jnp.int32), axis=2)
    my_owner = lax.dynamic_index_in_dim(table_owner, my_index, 0, keepdims=False)
    my_slot = lax.dynamic_index_in_dim(table_slot, my_index, 0, keepdims=False)
    my_target = slot_of[my_owner] * capacity + my_slot
    slot_ids = jnp.arange(capacity, dtype=jnp.int32)
    served = (table_owner == my_index)[:, :, None] & (
        table_slot[:, :, None] == slot_ids[None, None, :]
    )
    served_block = jnp.sum(jnp.where(served, table_offset[:, :, None], 0), axis=1)[range_at].reshape(-1)
    served_used = jnp.any(served, axis=1)[range_at].reshape(-1)
    outgoing = jnp.take(kv_blocks, served_block, axis=0)
    incoming = lax.all_to_all(outgoing, SEQ_AXES, split_axis=0, concat_axis=0, tiled=True)
    fetched = jnp.take(incoming, my_target, axis=0).reshape(blocks_here, NR, BS, 2 * head_cols)
    near_kv = jnp.concatenate([window, fetched], axis=1)
    near_groups = 3 + NR
    near_count = near_groups * BS
    query_heads = query_rows.reshape(blocks_here, BS, heads_here, DH)
    grad_heads = grad_rows.reshape(blocks_here, BS, heads_here, DH)
    near_keys = near_kv[..., :head_cols].reshape(blocks_here, near_groups, BS, heads_here, DH)
    near_values = near_kv[..., head_cols:].reshape(blocks_here, near_groups, BS, heads_here, DH)
    far_keys = global_kv[..., :head_cols].reshape(NG, BS, heads_here, DH)
    far_values = global_kv[..., head_cols:].reshape(NG, BS, heads_here, DH)
    scores = (
        jnp.concatenate(
            [
                jnp.einsum(
                    "bqhd,bgkhd->bhqgk", query_heads, near_keys, preferred_element_type=jnp.float32
                ).reshape(blocks_here, heads_here, BS, near_count),
                jnp.einsum(
                    "bqhd,gkhd->bhqgk", query_heads, far_keys, preferred_element_type=jnp.float32
                ).reshape(blocks_here, heads_here, BS, NG * BS),
            ],
            axis=3,
        )
        * inv_root
    )
    block_ids = my_index * blocks_here + jnp.arange(blocks_here, dtype=jnp.int32)
    usable = jnp.concatenate(
        [
            (block_ids > 0)[:, None],
            jnp.ones((blocks_here, 1), bool),
            (block_ids < total_blocks - 1)[:, None],
            jnp.ones((blocks_here, NR + NG), bool),
        ],
        axis=1,
    )
    column_ok = jnp.repeat(usable, BS, axis=1)[:, None, None, :]
    masked = jnp.where(column_ok, scores, -jnp.inf)
    row_max = jnp.max(masked, axis=3, keepdims=True)
    log_total = row_max + jnp.log(jnp.sum(jnp.exp(masked - row_max), axis=3, keepdims=True))
    probs_full = jnp.exp(masked - log_total)
    probs_half = probs_full.astype(jnp.bfloat16)
    near_probs = probs_half[..., :near_count].reshape(blocks_here, heads_here, BS, near_groups, BS)
    far_probs = probs_half[..., near_count:].reshape(blocks_here, heads_here, BS, NG, BS)
    outputs = jnp.einsum(
        "bhqgk,bgkhd->bqhd", near_probs, near_values, preferred_element_type=jnp.float32
    ) + jnp.einsum("bhqgk,gkhd->bqhd", far_probs, far_values, preferred_element_type=jnp.float32)
    row_dot = jnp.sum(grad_heads.astype(jnp.float32) * outputs, axis=3)
    dprobs = jnp.concatenate(
        [
            jnp.einsum(
                "bqhd,bgkhd->bhqgk", grad_heads, near_values, preferred_element_type=jnp.float32
            ).reshape(blocks_here, heads_here, BS, near_count),
            jnp.einsum(
                "bqhd,gkhd->bhqgk", grad_heads, far_values, preferred_element_type=jnp.float32
            ).reshape(blocks_here, heads_here, BS, NG * BS),
        ],
        axis=3,
    )
    dscores = probs_full * (dprobs - jnp.transpose(row_dot, (0, 2, 1))[..., None])
    ds_half = dscores.astype(jnp.bfloat16)
    near_ds = ds_half[..., :near_count].reshape(blocks_here, heads_here, BS, near_groups, BS)
    far_ds = ds_half[..., near_count:].reshape(blocks_here, heads_here, BS, NG, BS)
    query_grad = (
        (
            (
                jnp.einsum(
                    "bhqgk,bgkhd->bqhd", near_ds, near_keys, preferred_element_type=jnp.float32
                )
                + jnp.einsum(
                    "bhqgk,gkhd->bqhd", far_ds, far_keys, preferred_element_type=jnp.float32
                )
            )
            * inv_root
        )
        .astype(jnp.bfloat16)
        .reshape(tokens, head_cols)
    )

    def key_value_parts(ds_part, probs_part):
        key_part = (
            jnp.einsum(
                "bhqgk,bqhd->bgkhd", ds_part, query_heads, preferred_element_type=jnp.float32
            )
            * inv_root
        )
        value_part = jnp.einsum(
            "bhqgk,bqhd->bgkhd", probs_part, grad_heads, preferred_element_type=jnp.float32
        )
        out_shape = key_part.shape[:3] + (head_cols,)
        return jnp.concatenate([key_part.reshape(out_shape), value_part.reshape(out_shape)], axis=3)

    random_part = key_value_parts(near_ds[:, :, :, 3:], near_probs[:, :, :, 3:])
    random_part = random_part.astype(jnp.bfloat16).reshape(entries, BS, 2 * head_cols)
    back_rows = (
        jnp.zeros((devices * capacity, BS, 2 * head_cols), jnp.bfloat16)
        .at[my_target]
        .set(random_part)
    )
    arrived = lax.all_to_all(back_rows, SEQ_AXES, split_axis=0, concat_axis=0, tiled=True)
    window_part = key_value_parts(near_ds[:, :, :, :3], near_probs[:, :, :, :3])
    zero_block = jnp.zeros((1, BS, 2 * head_cols), jnp.float32)
    own_grad = (
        window_part[:, 1]
        + jnp.concatenate([window_part[1:, 0], zero_block], axis=0)
        + jnp.concatenate([zero_block, window_part[:-1, 2]], axis=0)
    )
    rims_out = jnp.concatenate([window_part[0, 0], window_part[blocks_here - 1, 2]], axis=0)
    rims_in = with_halo(rims_out.astype(jnp.bfloat16), ALL_AXES, halo_up, BS).astype(rims_out.dtype)
    own_grad = own_grad.at[0].add(rims_in[:BS]).at[blocks_here - 1].add(rims_in[3 * BS :])
    far_key = (
        jnp.einsum("bhqgk,bqhd->gkhd", far_ds, query_heads, preferred_element_type=jnp.float32)
        * inv_root
    )
    far_value = jnp.einsum(
        "bhqgk,bqhd->gkhd", far_probs, grad_heads, preferred_element_type=jnp.float32
    )
    far_part = jnp.concatenate(
        [far_key.reshape(NG, BS, head_cols), far_value.reshape(NG, BS, head_cols)], axis=2
    )
    far_sum = all_sum(far_part, SEQ_AXES)
    here_ids = jnp.arange(blocks_here, dtype=jnp.int32)
    own_global = (
        (global_owner == my_index)[None, :] & (global_offset[None, :] == here_ids[:, None])
    ).astype(jnp.float32)
    own_grad = own_grad + jnp.einsum(
        "jg,gkc->jkc", own_global, far_sum, precision=lax.Precision.HIGHEST
    )
    weights = (served_used[None, :] & (served_block[None, :] == here_ids[:, None])).astype(
        jnp.bfloat16
    )
    own_grad = own_grad + jnp.einsum(
        "jr,rkc->jkc", weights, arrived, preferred_element_type=jnp.float32
    )
    key_grad = own_grad[..., :head_cols].astype(jnp.bfloat16).reshape(tokens, head_cols)
    value_grad = own_grad[..., head_cols:].astype(jnp.bfloat16).reshape(tokens, head_cols)
    outs = send_home(jnp.stack([query_grad, key_grad, value_grad]))
    return outs[0], outs[1], outs[2]


def solution(mesh):
    side = mesh.devices.shape[1] // 2
    grid = mesh.devices.reshape(-1, mesh.devices.shape[0] // (side * side), side, side, 2)
    cube = jax.sharding.Mesh(grid, ("zh", "zl", "y", "x", "core"))
    rows = ("zh", "zl", "y", "x", "core")
    placed = (P(rows, None),) * 4 + (P(), P())
    out = P(("zh", "zl", "y"), ("x", "core"))
    return jax.shard_map(
        per_device,
        mesh=cube,
        in_specs=placed,
        out_specs=(out, out, out),
        check_vma=False,
    )
```

```python
import math

import jax
import numpy as np
import jax.numpy as jnp
from jax import lax
from jax.sharding import PartitionSpec as P

DH = 128
BS = 32
NR = 3
NG = 4


def with_halo(x, axis, up, width):
    down = [(j, i) for i, j in up]
    length = x.shape[0]
    before = lax.ppermute(x[length - width :], axis, up)
    after = lax.ppermute(x[:width], axis, down)
    return jnp.concatenate([before, x, after], axis=0)


def chunk_sum(x, axis):
    peers = lax.axis_size(axis)
    parts = lax.all_to_all(x.reshape(peers, -1), axis, split_axis=0, concat_axis=0, tiled=True)
    return jnp.sum(parts.astype(jnp.float32), axis=0)


def chunk_share(chunk, axis, shape, dtype):
    peers = lax.axis_size(axis)
    copies = jnp.broadcast_to(chunk.astype(dtype)[None], (peers,) + chunk.shape)
    return lax.all_to_all(copies, axis, split_axis=0, concat_axis=0, tiled=True).reshape(shape)


def all_sum(x, axis):
    return chunk_share(chunk_sum(x, axis), axis, x.shape, x.dtype)


SEQ_AXES = ("zl", "y", "x")
SWAP_AXES = ("zh", "x")


ALL_AXES = ("zh", "zl", "y", "x", "core")


def move_slabs(x, forward):
    side = lax.axis_size("x")
    pairs = [(a * side + b, ((b - a) % side) * side + b) for a in range(side) for b in range(side)]
    if not forward:
        pairs = [(j, i) for i, j in pairs]
    return lax.ppermute(x, SWAP_AXES, pairs)


def shift_columns(x):
    side = lax.axis_size("x")
    pairs = [(a * side + b, a * side + (b - a) % side) for a in range(side) for b in range(side)]
    return lax.ppermute(x, SWAP_AXES, pairs)


def send_home(x):
    side = lax.axis_size("x")
    pairs = [(b * side + x, ((x - b) % side) * side + b) for b in range(side) for x in range(side)]
    return lax.ppermute(x, SWAP_AXES, pairs)


def layout_tables(sizes):
    hz, lz, ly, lx, cores = sizes
    ranges = lz * ly * lx
    slot = np.zeros((hz, ranges), np.int32)
    for b in range(hz):
        for r in range(ranges):
            slot[b, r] = ((r // ly) % lz) * (ly * lx) + (r % ly) * lx + (r // (lz * ly) + b) % lx
    up = []
    for b in range(hz):
        for c in range(cores):
            for r in range(ranges - 1):
                here, there = slot[b, r], slot[b, r + 1]
                up.append(((b * ranges + here) * cores + c, (b * ranges + there) * cores + c))
    return slot, np.argsort(slot, axis=1).astype(np.int32), up


def per_device(queries, key_states, value_states, out_grad, random_blocks, global_blocks):
    groups = lax.axis_size(("x", "core"))
    rows_in, cols_in = queries.shape
    stacked = jnp.stack([queries, key_states, value_states, out_grad], axis=1)
    sizes = tuple(lax.axis_size(a) for a in ALL_AXES)
    stacked = stacked.reshape(rows_in, 4, sizes[3], groups // sizes[3], cols_in // groups)
    stacked = jnp.roll(stacked, lax.axis_index("zh"), axis=2)
    stacked = stacked.reshape(rows_in, 4, groups, cols_in // groups)
    stacked = lax.all_to_all(stacked, ("x", "core"), split_axis=2, concat_axis=0, tiled=True)
    stacked = move_slabs(stacked, True)
    query_rows, key_rows, value_rows, grad_rows = (stacked[:, i, 0] for i in range(4))
    tokens = query_rows.shape[0]
    head_cols = query_rows.shape[1]
    heads_here = head_cols // DH
    blocks_here = tokens // BS
    lz, ly, lx = (lax.axis_size(a) for a in SEQ_AXES)
    devices = lz * ly * lx
    slab = lax.axis_index("zh")
    my_index = ((lax.axis_index("x") - slab) % lx * lz + lax.axis_index("zl")) * ly + lax.axis_index("y")
    slot_table, range_table, halo_up = layout_tables(sizes)
    slot_of = jnp.asarray(slot_table)[slab]
    range_at = jnp.asarray(range_table)[slab]
    total_blocks = devices * blocks_here
    entries = blocks_here * NR
    capacity = (entries + devices - 1) // devices
    inv_root = 1.0 / math.sqrt(DH)
    kv_rows = jnp.concatenate([key_rows, value_rows], axis=1)
    kv_blocks = kv_rows.reshape(blocks_here, BS, 2 * head_cols)
    extended = with_halo(kv_rows, ALL_AXES, halo_up, BS)
    extended = extended.reshape(blocks_here + 2, BS, 2 * head_cols)
    window = jnp.stack(
        [extended[:blocks_here], extended[1 : blocks_here + 1], extended[2:]], axis=1
    )
    global_owner = global_blocks // blocks_here
    global_offset = global_blocks % blocks_here
    owned = jnp.take(kv_blocks, global_offset, axis=0)
    owned = jnp.where((global_owner == my_index)[:, None, None], owned, jnp.zeros_like(owned))
    global_kv = all_sum(owned, SEQ_AXES)
    entry_table = random_blocks.reshape(devices, entries)
    table_owner = entry_table // blocks_here
    table_offset = entry_table % blocks_here
    positions = jnp.arange(entries, dtype=jnp.int32)
    before = positions[None, :] < positions[:, None]
    matches = (table_owner[:, :, None] == table_owner[:, None, :]) & before[None]
    table_slot = jnp.sum(matches.astype(jnp.int32), axis=2)
    my_owner = lax.dynamic_index_in_dim(table_owner, my_index, 0, keepdims=False)
    my_slot = lax.dynamic_index_in_dim(table_slot, my_index, 0, keepdims=False)
    my_target = slot_of[my_owner] * capacity + my_slot
    slot_ids = jnp.arange(capacity, dtype=jnp.int32)
    served = (table_owner == my_index)[:, :, None] & (
        table_slot[:, :, None] == slot_ids[None, None, :]
    )
    served_block = jnp.sum(jnp.where(served, table_offset[:, :, None], 0), axis=1)[range_at].reshape(-1)
    served_used = jnp.any(served, axis=1)[range_at].reshape(-1)
    outgoing = jnp.take(kv_blocks, served_block, axis=0)
    incoming = lax.all_to_all(outgoing, SEQ_AXES, split_axis=0, concat_axis=0, tiled=True)
    fetched = jnp.take(incoming, my_target, axis=0).reshape(blocks_here, NR, BS, 2 * head_cols)
    near_kv = jnp.concatenate([window, fetched], axis=1)
    near_groups = 3 + NR
    near_count = near_groups * BS
    query_heads = query_rows.reshape(blocks_here, BS, heads_here, DH)
    grad_heads = grad_rows.reshape(blocks_here, BS, heads_here, DH)
    near_keys = near_kv[..., :head_cols].reshape(blocks_here, near_groups, BS, heads_here, DH)
    near_values = near_kv[..., head_cols:].reshape(blocks_here, near_groups, BS, heads_here, DH)
    far_keys = global_kv[..., :head_cols].reshape(NG, BS, heads_here, DH)
    far_values = global_kv[..., head_cols:].reshape(NG, BS, heads_here, DH)
    scores = (
        jnp.concatenate(
            [
                jnp.einsum(
                    "bqhd,bgkhd->bhqgk", query_heads, near_keys, preferred_element_type=jnp.float32
                ).reshape(blocks_here, heads_here, BS, near_count),
                jnp.einsum(
                    "bqhd,gkhd->bhqgk", query_heads, far_keys, preferred_element_type=jnp.float32
                ).reshape(blocks_here, heads_here, BS, NG * BS),
            ],
            axis=3,
        )
        * inv_root
    )
    block_ids = my_index * blocks_here + jnp.arange(blocks_here, dtype=jnp.int32)
    usable = jnp.concatenate(
        [
            (block_ids > 0)[:, None],
            jnp.ones((blocks_here, 1), bool),
            (block_ids < total_blocks - 1)[:, None],
            jnp.ones((blocks_here, NR + NG), bool),
        ],
        axis=1,
    )
    column_ok = jnp.repeat(usable, BS, axis=1)[:, None, None, :]
    masked = jnp.where(column_ok, scores, -jnp.inf)
    row_max = jnp.max(masked, axis=3, keepdims=True)
    log_total = row_max + jnp.log(jnp.sum(jnp.exp(masked - row_max), axis=3, keepdims=True))
    probs_full = jnp.exp(masked - log_total)
    probs_half = probs_full.astype(jnp.bfloat16)
    near_probs = probs_half[..., :near_count].reshape(blocks_here, heads_here, BS, near_groups, BS)
    far_probs = probs_half[..., near_count:].reshape(blocks_here, heads_here, BS, NG, BS)
    outputs = jnp.einsum(
        "bhqgk,bgkhd->bqhd", near_probs, near_values, preferred_element_type=jnp.float32
    ) + jnp.einsum("bhqgk,gkhd->bqhd", far_probs, far_values, preferred_element_type=jnp.float32)
    row_dot = jnp.sum(grad_heads.astype(jnp.float32) * outputs, axis=3)
    dprobs = jnp.concatenate(
        [
            jnp.einsum(
                "bqhd,bgkhd->bhqgk", grad_heads, near_values, preferred_element_type=jnp.float32
            ).reshape(blocks_here, heads_here, BS, near_count),
            jnp.einsum(
                "bqhd,gkhd->bhqgk", grad_heads, far_values, preferred_element_type=jnp.float32
            ).reshape(blocks_here, heads_here, BS, NG * BS),
        ],
        axis=3,
    )
    dscores = probs_full * (dprobs - jnp.transpose(row_dot, (0, 2, 1))[..., None])
    ds_half = dscores.astype(jnp.bfloat16)
    near_ds = ds_half[..., :near_count].reshape(blocks_here, heads_here, BS, near_groups, BS)
    far_ds = ds_half[..., near_count:].reshape(blocks_here, heads_here, BS, NG, BS)
    query_grad = (
        (
            (
                jnp.einsum(
                    "bhqgk,bgkhd->bqhd", near_ds, near_keys, preferred_element_type=jnp.float32
                )
                + jnp.einsum(
                    "bhqgk,gkhd->bqhd", far_ds, far_keys, preferred_element_type=jnp.float32
                )
            )
            * inv_root
        )
        .astype(jnp.bfloat16)
        .reshape(tokens, head_cols)
    )

    def key_value_parts(ds_part, probs_part):
        key_part = (
            jnp.einsum(
                "bhqgk,bqhd->bgkhd", ds_part, query_heads, preferred_element_type=jnp.float32
            )
            * inv_root
        )
        value_part = jnp.einsum(
            "bhqgk,bqhd->bgkhd", probs_part, grad_heads, preferred_element_type=jnp.float32
        )
        out_shape = key_part.shape[:3] + (head_cols,)
        return jnp.concatenate([key_part.reshape(out_shape), value_part.reshape(out_shape)], axis=3)

    random_part = key_value_parts(near_ds[:, :, :, 3:], near_probs[:, :, :, 3:])
    random_part = random_part.astype(jnp.bfloat16).reshape(entries, BS, 2 * head_cols)
    back_rows = (
        jnp.zeros((devices * capacity, BS, 2 * head_cols), jnp.bfloat16)
        .at[my_target]
        .set(random_part)
    )
    arrived = lax.all_to_all(back_rows, SEQ_AXES, split_axis=0, concat_axis=0, tiled=True)
    window_part = key_value_parts(near_ds[:, :, :, :3], near_probs[:, :, :, :3])
    zero_block = jnp.zeros((1, BS, 2 * head_cols), jnp.float32)
    own_grad = (
        window_part[:, 1]
        + jnp.concatenate([window_part[1:, 0], zero_block], axis=0)
        + jnp.concatenate([zero_block, window_part[:-1, 2]], axis=0)
    )
    rims_out = jnp.concatenate([window_part[0, 0], window_part[blocks_here - 1, 2]], axis=0)
    rims_in = with_halo(rims_out.astype(jnp.bfloat16), ALL_AXES, halo_up, BS).astype(rims_out.dtype)
    own_grad = own_grad.at[0].add(rims_in[:BS]).at[blocks_here - 1].add(rims_in[3 * BS :])
    far_key = (
        jnp.einsum("bhqgk,bqhd->gkhd", far_ds, query_heads, preferred_element_type=jnp.float32)
        * inv_root
    )
    far_value = jnp.einsum(
        "bhqgk,bqhd->gkhd", far_probs, grad_heads, preferred_element_type=jnp.float32
    )
    far_part = jnp.concatenate(
        [far_key.reshape(NG, BS, head_cols), far_value.reshape(NG, BS, head_cols)], axis=2
    )
    far_part, arrived = lax.optimization_barrier((far_part, arrived))
    far_sum = all_sum(far_part, SEQ_AXES)
    here_ids = jnp.arange(blocks_here, dtype=jnp.int32)
    own_global = (
        (global_owner == my_index)[None, :] & (global_offset[None, :] == here_ids[:, None])
    ).astype(jnp.float32)
    own_grad = own_grad + jnp.einsum(
        "jg,gkc->jkc", own_global, far_sum, precision=lax.Precision.HIGHEST
    )
    weights = (served_used[None, :] & (served_block[None, :] == here_ids[:, None])).astype(
        jnp.bfloat16
    )
    own_grad = own_grad + jnp.einsum(
        "jr,rkc->jkc", weights, arrived, preferred_element_type=jnp.float32
    )
    key_grad = own_grad[..., :head_cols].astype(jnp.bfloat16).reshape(tokens, head_cols)
    value_grad = own_grad[..., head_cols:].astype(jnp.bfloat16).reshape(tokens, head_cols)
    outs = send_home(jnp.stack([query_grad, key_grad, value_grad]))
    return outs[0], outs[1], outs[2]


def solution(mesh):
    side = mesh.devices.shape[1] // 2
    grid = mesh.devices.reshape(-1, mesh.devices.shape[0] // (side * side), side, side, 2)
    cube = jax.sharding.Mesh(grid, ("zh", "zl", "y", "x", "core"))
    rows = ("zh", "zl", "y", "x", "core")
    placed = (P(rows, None),) * 4 + (P(), P())
    out = P(("zh", "zl", "y"), ("x", "core"))
    return jax.shard_map(
        per_device,
        mesh=cube,
        in_specs=placed,
        out_specs=(out, out, out),
        check_vma=False,
    )
```

```python
import math

import jax
import numpy as np
import jax.numpy as jnp
from jax import lax
from jax.sharding import PartitionSpec as P

DH = 128
BS = 32
NR = 3
NG = 4


def with_halo(x, axis, up, width):
    down = [(j, i) for i, j in up]
    length = x.shape[0]
    before = lax.ppermute(x[length - width :], axis, up)
    after = lax.ppermute(x[:width], axis, down)
    return jnp.concatenate([before, x, after], axis=0)


def chunk_sum(x, axis):
    peers = lax.axis_size(axis)
    parts = lax.all_to_all(x.reshape(peers, -1), axis, split_axis=0, concat_axis=0, tiled=True)
    return jnp.sum(parts.astype(jnp.float32), axis=0)


def chunk_share(chunk, axis, shape, dtype):
    peers = lax.axis_size(axis)
    copies = jnp.broadcast_to(chunk.astype(dtype)[None], (peers,) + chunk.shape)
    return lax.all_to_all(copies, axis, split_axis=0, concat_axis=0, tiled=True).reshape(shape)


def all_sum(x, axis):
    return chunk_share(chunk_sum(x, axis), axis, x.shape, x.dtype)


SEQ_AXES = ("zl", "y", "x")
SWAP_AXES = ("zh", "x")


ALL_AXES = ("zh", "zl", "y", "x", "core")


def move_slabs(x, forward):
    side = lax.axis_size("x")
    pairs = [(a * side + b, ((b - a) % side) * side + b) for a in range(side) for b in range(side)]
    if not forward:
        pairs = [(j, i) for i, j in pairs]
    return lax.ppermute(x, SWAP_AXES, pairs)


def shift_columns(x):
    side = lax.axis_size("x")
    pairs = [(a * side + b, a * side + (b - a) % side) for a in range(side) for b in range(side)]
    return lax.ppermute(x, SWAP_AXES, pairs)


def send_home(x):
    side = lax.axis_size("x")
    pairs = [(b * side + x, ((x - b) % side) * side + b) for b in range(side) for x in range(side)]
    return lax.ppermute(x, SWAP_AXES, pairs)


def layout_tables(sizes):
    hz, lz, ly, lx, cores = sizes
    ranges = lz * ly * lx
    slot = np.zeros((hz, ranges), np.int32)
    for b in range(hz):
        for r in range(ranges):
            slot[b, r] = ((r // ly) % lz) * (ly * lx) + (r % ly) * lx + (r // (lz * ly) + b) % lx
    up = []
    for b in range(hz):
        for c in range(cores):
            for r in range(ranges - 1):
                here, there = slot[b, r], slot[b, r + 1]
                up.append(((b * ranges + here) * cores + c, (b * ranges + there) * cores + c))
    return slot, np.argsort(slot, axis=1).astype(np.int32), up


def per_device(queries, key_states, value_states, out_grad, random_blocks, global_blocks):
    groups = lax.axis_size(("x", "core"))
    rows_in, cols_in = queries.shape
    stacked = jnp.stack([queries, key_states, value_states, out_grad], axis=1)
    sizes = tuple(lax.axis_size(a) for a in ALL_AXES)
    stacked = stacked.reshape(rows_in, 4, sizes[3], groups // sizes[3], cols_in // groups)
    stacked = jnp.roll(stacked, lax.axis_index("zh"), axis=2)
    stacked = stacked.reshape(rows_in, 4, groups, cols_in // groups)
    stacked = lax.all_to_all(stacked, ("x", "core"), split_axis=2, concat_axis=0, tiled=True)
    stacked = move_slabs(stacked, True)
    query_rows, key_rows, value_rows, grad_rows = (stacked[:, i, 0] for i in range(4))
    tokens = query_rows.shape[0]
    head_cols = query_rows.shape[1]
    heads_here = head_cols // DH
    blocks_here = tokens // BS
    lz, ly, lx = (lax.axis_size(a) for a in SEQ_AXES)
    devices = lz * ly * lx
    slab = lax.axis_index("zh")
    my_index = ((lax.axis_index("x") - slab) % lx * lz + lax.axis_index("zl")) * ly + lax.axis_index("y")
    slot_table, range_table, halo_up = layout_tables(sizes)
    slot_of = jnp.asarray(slot_table)[slab]
    range_at = jnp.asarray(range_table)[slab]
    total_blocks = devices * blocks_here
    entries = blocks_here * NR
    capacity = (entries + devices - 1) // devices
    inv_root = 1.0 / math.sqrt(DH)
    kv_rows = jnp.concatenate([key_rows, value_rows], axis=1)
    kv_blocks = kv_rows.reshape(blocks_here, BS, 2 * head_cols)
    extended = with_halo(kv_rows, ALL_AXES, halo_up, BS)
    extended = extended.reshape(blocks_here + 2, BS, 2 * head_cols)
    window = jnp.stack(
        [extended[:blocks_here], extended[1 : blocks_here + 1], extended[2:]], axis=1
    )
    global_owner = global_blocks // blocks_here
    global_offset = global_blocks % blocks_here
    owned = jnp.take(kv_blocks, global_offset, axis=0)
    owned = jnp.where((global_owner == my_index)[:, None, None], owned, jnp.zeros_like(owned))
    global_kv = all_sum(owned, SEQ_AXES)
    entry_table = random_blocks.reshape(devices, entries)
    table_owner = entry_table // blocks_here
    table_offset = entry_table % blocks_here
    positions = jnp.arange(entries, dtype=jnp.int32)
    before = positions[None, :] < positions[:, None]
    matches = (table_owner[:, :, None] == table_owner[:, None, :]) & before[None]
    table_slot = jnp.sum(matches.astype(jnp.int32), axis=2)
    my_owner = lax.dynamic_index_in_dim(table_owner, my_index, 0, keepdims=False)
    my_slot = lax.dynamic_index_in_dim(table_slot, my_index, 0, keepdims=False)
    my_target = slot_of[my_owner] * capacity + my_slot
    slot_ids = jnp.arange(capacity, dtype=jnp.int32)
    served = (table_owner == my_index)[:, :, None] & (
        table_slot[:, :, None] == slot_ids[None, None, :]
    )
    served_block = jnp.sum(jnp.where(served, table_offset[:, :, None], 0), axis=1)[range_at].reshape(-1)
    served_used = jnp.any(served, axis=1)[range_at].reshape(-1)
    outgoing = jnp.take(kv_blocks, served_block, axis=0)
    incoming = lax.all_to_all(outgoing, SEQ_AXES, split_axis=0, concat_axis=0, tiled=True)
    fetched = jnp.take(incoming, my_target, axis=0).reshape(blocks_here, NR, BS, 2 * head_cols)
    near_kv = jnp.concatenate([window, fetched], axis=1)
    near_groups = 3 + NR
    near_count = near_groups * BS
    query_heads = query_rows.reshape(blocks_here, BS, heads_here, DH)
    grad_heads = grad_rows.reshape(blocks_here, BS, heads_here, DH)
    near_keys = near_kv[..., :head_cols].reshape(blocks_here, near_groups, BS, heads_here, DH)
    near_values = near_kv[..., head_cols:].reshape(blocks_here, near_groups, BS, heads_here, DH)
    far_keys = global_kv[..., :head_cols].reshape(NG, BS, heads_here, DH)
    far_values = global_kv[..., head_cols:].reshape(NG, BS, heads_here, DH)
    scores = (
        jnp.concatenate(
            [
                jnp.einsum(
                    "bqhd,bgkhd->bhqgk", query_heads, near_keys, preferred_element_type=jnp.float32
                ).reshape(blocks_here, heads_here, BS, near_count),
                jnp.einsum(
                    "bqhd,gkhd->bhqgk", query_heads, far_keys, preferred_element_type=jnp.float32
                ).reshape(blocks_here, heads_here, BS, NG * BS),
            ],
            axis=3,
        )
        * inv_root
    )
    block_ids = my_index * blocks_here + jnp.arange(blocks_here, dtype=jnp.int32)
    usable = jnp.concatenate(
        [
            (block_ids > 0)[:, None],
            jnp.ones((blocks_here, 1), bool),
            (block_ids < total_blocks - 1)[:, None],
            jnp.ones((blocks_here, NR + NG), bool),
        ],
        axis=1,
    )
    column_ok = jnp.repeat(usable, BS, axis=1)[:, None, None, :]
    masked = jnp.where(column_ok, scores, -jnp.inf)
    row_max = jnp.max(masked, axis=3, keepdims=True)
    log_total = row_max + jnp.log(jnp.sum(jnp.exp(masked - row_max), axis=3, keepdims=True))
    probs_full = jnp.exp(masked - log_total)
    probs_half = probs_full.astype(jnp.bfloat16)
    near_probs = probs_half[..., :near_count].reshape(blocks_here, heads_here, BS, near_groups, BS)
    far_probs = probs_half[..., near_count:].reshape(blocks_here, heads_here, BS, NG, BS)
    outputs = jnp.einsum(
        "bhqgk,bgkhd->bqhd", near_probs, near_values, preferred_element_type=jnp.float32
    ) + jnp.einsum("bhqgk,gkhd->bqhd", far_probs, far_values, preferred_element_type=jnp.float32)
    row_dot = jnp.sum(grad_heads.astype(jnp.float32) * outputs, axis=3)
    dprobs = jnp.concatenate(
        [
            jnp.einsum(
                "bqhd,bgkhd->bhqgk", grad_heads, near_values, preferred_element_type=jnp.float32
            ).reshape(blocks_here, heads_here, BS, near_count),
            jnp.einsum(
                "bqhd,gkhd->bhqgk", grad_heads, far_values, preferred_element_type=jnp.float32
            ).reshape(blocks_here, heads_here, BS, NG * BS),
        ],
        axis=3,
    )
    dscores = probs_full * (dprobs - jnp.transpose(row_dot, (0, 2, 1))[..., None])
    ds_half = dscores.astype(jnp.bfloat16)
    near_ds = ds_half[..., :near_count].reshape(blocks_here, heads_here, BS, near_groups, BS)
    far_ds = ds_half[..., near_count:].reshape(blocks_here, heads_here, BS, NG, BS)
    query_grad = (
        (
            (
                jnp.einsum(
                    "bhqgk,bgkhd->bqhd", near_ds, near_keys, preferred_element_type=jnp.float32
                )
                + jnp.einsum(
                    "bhqgk,gkhd->bqhd", far_ds, far_keys, preferred_element_type=jnp.float32
                )
            )
            * inv_root
        )
        .astype(jnp.bfloat16)
        .reshape(tokens, head_cols)
    )

    def key_value_parts(ds_part, probs_part):
        key_part = (
            jnp.einsum(
                "bhqgk,bqhd->bgkhd", ds_part, query_heads, preferred_element_type=jnp.float32
            )
            * inv_root
        )
        value_part = jnp.einsum(
            "bhqgk,bqhd->bgkhd", probs_part, grad_heads, preferred_element_type=jnp.float32
        )
        out_shape = key_part.shape[:3] + (head_cols,)
        return jnp.concatenate([key_part.reshape(out_shape), value_part.reshape(out_shape)], axis=3)

    random_part = key_value_parts(near_ds[:, :, :, 3:], near_probs[:, :, :, 3:])
    random_part = random_part.astype(jnp.bfloat16).reshape(entries, BS, 2 * head_cols)
    back_rows = (
        jnp.zeros((devices * capacity, BS, 2 * head_cols), jnp.bfloat16)
        .at[my_target]
        .set(random_part)
    )
    query_home, back_rows = lax.optimization_barrier((send_home(query_grad), back_rows))
    arrived = lax.all_to_all(back_rows, SEQ_AXES, split_axis=0, concat_axis=0, tiled=True)
    window_part = key_value_parts(near_ds[:, :, :, :3], near_probs[:, :, :, :3])
    zero_block = jnp.zeros((1, BS, 2 * head_cols), jnp.float32)
    own_grad = (
        window_part[:, 1]
        + jnp.concatenate([window_part[1:, 0], zero_block], axis=0)
        + jnp.concatenate([zero_block, window_part[:-1, 2]], axis=0)
    )
    rims_out = jnp.concatenate([window_part[0, 0], window_part[blocks_here - 1, 2]], axis=0)
    rims_in = with_halo(rims_out.astype(jnp.bfloat16), ALL_AXES, halo_up, BS).astype(rims_out.dtype)
    own_grad = own_grad.at[0].add(rims_in[:BS]).at[blocks_here - 1].add(rims_in[3 * BS :])
    far_key = (
        jnp.einsum("bhqgk,bqhd->gkhd", far_ds, query_heads, preferred_element_type=jnp.float32)
        * inv_root
    )
    far_value = jnp.einsum(
        "bhqgk,bqhd->gkhd", far_probs, grad_heads, preferred_element_type=jnp.float32
    )
    far_part = jnp.concatenate(
        [far_key.reshape(NG, BS, head_cols), far_value.reshape(NG, BS, head_cols)], axis=2
    )
    far_sum = all_sum(far_part, SEQ_AXES)
    here_ids = jnp.arange(blocks_here, dtype=jnp.int32)
    own_global = (
        (global_owner == my_index)[None, :] & (global_offset[None, :] == here_ids[:, None])
    ).astype(jnp.float32)
    own_grad = own_grad + jnp.einsum(
        "jg,gkc->jkc", own_global, far_sum, precision=lax.Precision.HIGHEST
    )
    weights = (served_used[None, :] & (served_block[None, :] == here_ids[:, None])).astype(
        jnp.bfloat16
    )
    own_grad = own_grad + jnp.einsum(
        "jr,rkc->jkc", weights, arrived, preferred_element_type=jnp.float32
    )
    key_grad = own_grad[..., :head_cols].astype(jnp.bfloat16).reshape(tokens, head_cols)
    value_grad = own_grad[..., head_cols:].astype(jnp.bfloat16).reshape(tokens, head_cols)
    outs = send_home(jnp.stack([key_grad, value_grad]))
    return query_home, outs[0], outs[1]


def solution(mesh):
    side = mesh.devices.shape[1] // 2
    grid = mesh.devices.reshape(-1, mesh.devices.shape[0] // (side * side), side, side, 2)
    cube = jax.sharding.Mesh(grid, ("zh", "zl", "y", "x", "core"))
    rows = ("zh", "zl", "y", "x", "core")
    placed = (P(rows, None),) * 4 + (P(), P())
    out = P(("zh", "zl", "y"), ("x", "core"))
    return jax.shard_map(
        per_device,
        mesh=cube,
        in_specs=placed,
        out_specs=(out, out, out),
        check_vma=False,
    )
```

```python
import math

import jax
import numpy as np
import jax.numpy as jnp
from jax import lax
from jax.sharding import PartitionSpec as P

DH = 128
BS = 32
NR = 3
NG = 4


def with_halo(x, axis, up, width):
    down = [(j, i) for i, j in up]
    length = x.shape[0]
    before = lax.ppermute(x[length - width :], axis, up)
    after = lax.ppermute(x[:width], axis, down)
    return jnp.concatenate([before, x, after], axis=0)


def chunk_sum(x, axis):
    peers = lax.axis_size(axis)
    parts = lax.all_to_all(x.reshape(peers, -1), axis, split_axis=0, concat_axis=0, tiled=True)
    return jnp.sum(parts.astype(jnp.float32), axis=0)


def chunk_share(chunk, axis, shape, dtype):
    peers = lax.axis_size(axis)
    copies = jnp.broadcast_to(chunk.astype(dtype)[None], (peers,) + chunk.shape)
    return lax.all_to_all(copies, axis, split_axis=0, concat_axis=0, tiled=True).reshape(shape)


def all_sum(x, axis):
    return chunk_share(chunk_sum(x, axis), axis, x.shape, x.dtype)


SEQ_AXES = ("zl", "y", "x")
SWAP_AXES = ("zh", "x")


ALL_AXES = ("zh", "zl", "y", "x", "core")


def move_slabs(x, forward):
    side = lax.axis_size("x")
    pairs = [(a * side + b, ((b - a) % side) * side + b) for a in range(side) for b in range(side)]
    if not forward:
        pairs = [(j, i) for i, j in pairs]
    return lax.ppermute(x, SWAP_AXES, pairs)


def shift_columns(x):
    side = lax.axis_size("x")
    pairs = [(a * side + b, a * side + (b - a) % side) for a in range(side) for b in range(side)]
    return lax.ppermute(x, SWAP_AXES, pairs)


def send_home(x):
    side = lax.axis_size("x")
    pairs = [(b * side + x, ((x - b) % side) * side + b) for b in range(side) for x in range(side)]
    return lax.ppermute(x, SWAP_AXES, pairs)


def layout_tables(sizes):
    hz, lz, ly, lx, cores = sizes
    ranges = lz * ly * lx
    slot = np.zeros((hz, ranges), np.int32)
    for b in range(hz):
        for r in range(ranges):
            slot[b, r] = ((r // ly) % lz) * (ly * lx) + (r % ly) * lx + (r // (lz * ly) + b) % lx
    up = []
    for b in range(hz):
        for c in range(cores):
            for r in range(ranges - 1):
                here, there = slot[b, r], slot[b, r + 1]
                up.append(((b * ranges + here) * cores + c, (b * ranges + there) * cores + c))
    return slot, np.argsort(slot, axis=1).astype(np.int32), up


def per_device(queries, key_states, value_states, out_grad, random_blocks, global_blocks):
    groups = lax.axis_size(("x", "core"))
    rows_in, cols_in = queries.shape
    stacked = jnp.stack([queries, key_states, value_states, out_grad], axis=1)
    sizes = tuple(lax.axis_size(a) for a in ALL_AXES)
    stacked = stacked.reshape(rows_in, 4, sizes[3], groups // sizes[3], cols_in // groups)
    lanes = jnp.arange(sizes[3], dtype=jnp.int32)
    stacked = jnp.take(stacked, (lanes - lax.axis_index("zh")) % sizes[3], axis=2)
    stacked = stacked.reshape(rows_in, 4, groups, cols_in // groups)
    stacked = lax.all_to_all(stacked, ("x", "core"), split_axis=2, concat_axis=0, tiled=True)
    stacked = move_slabs(stacked, True)
    query_rows, key_rows, value_rows, grad_rows = (stacked[:, i, 0] for i in range(4))
    tokens = query_rows.shape[0]
    head_cols = query_rows.shape[1]
    heads_here = head_cols // DH
    blocks_here = tokens // BS
    lz, ly, lx = (lax.axis_size(a) for a in SEQ_AXES)
    devices = lz * ly * lx
    slab = lax.axis_index("zh")
    my_index = ((lax.axis_index("x") - slab) % lx * lz + lax.axis_index("zl")) * ly + lax.axis_index("y")
    slot_table, range_table, halo_up = layout_tables(sizes)
    slot_of = jnp.asarray(slot_table)[slab]
    range_at = jnp.asarray(range_table)[slab]
    total_blocks = devices * blocks_here
    entries = blocks_here * NR
    capacity = (entries + devices - 1) // devices
    inv_root = 1.0 / math.sqrt(DH)
    kv_rows = jnp.concatenate([key_rows, value_rows], axis=1)
    kv_blocks = kv_rows.reshape(blocks_here, BS, 2 * head_cols)
    extended = with_halo(kv_rows, ALL_AXES, halo_up, BS)
    extended = extended.reshape(blocks_here + 2, BS, 2 * head_cols)
    window = jnp.stack(
        [extended[:blocks_here], extended[1 : blocks_here + 1], extended[2:]], axis=1
    )
    global_owner = global_blocks // blocks_here
    global_offset = global_blocks % blocks_here
    owned = jnp.take(kv_blocks, global_offset, axis=0)
    owned = jnp.where((global_owner == my_index)[:, None, None], owned, jnp.zeros_like(owned))
    global_kv = all_sum(owned, SEQ_AXES)
    entry_table = random_blocks.reshape(devices, entries)
    table_owner = entry_table // blocks_here
    table_offset = entry_table % blocks_here
    positions = jnp.arange(entries, dtype=jnp.int32)
    before = positions[None, :] < positions[:, None]
    matches = (table_owner[:, :, None] == table_owner[:, None, :]) & before[None]
    table_slot = jnp.sum(matches.astype(jnp.int32), axis=2)
    my_owner = lax.dynamic_index_in_dim(table_owner, my_index, 0, keepdims=False)
    my_slot = lax.dynamic_index_in_dim(table_slot, my_index, 0, keepdims=False)
    my_target = slot_of[my_owner] * capacity + my_slot
    slot_ids = jnp.arange(capacity, dtype=jnp.int32)
    served = (table_owner == my_index)[:, :, None] & (
        table_slot[:, :, None] == slot_ids[None, None, :]
    )
    served_block = jnp.sum(jnp.where(served, table_offset[:, :, None], 0), axis=1)[range_at].reshape(-1)
    served_used = jnp.any(served, axis=1)[range_at].reshape(-1)
    outgoing = jnp.take(kv_blocks, served_block, axis=0)
    incoming = lax.all_to_all(outgoing, SEQ_AXES, split_axis=0, concat_axis=0, tiled=True)
    fetched = jnp.take(incoming, my_target, axis=0).reshape(blocks_here, NR, BS, 2 * head_cols)
    near_kv = jnp.concatenate([window, fetched], axis=1)
    near_groups = 3 + NR
    near_count = near_groups * BS
    query_heads = query_rows.reshape(blocks_here, BS, heads_here, DH)
    grad_heads = grad_rows.reshape(blocks_here, BS, heads_here, DH)
    near_keys = near_kv[..., :head_cols].reshape(blocks_here, near_groups, BS, heads_here, DH)
    near_values = near_kv[..., head_cols:].reshape(blocks_here, near_groups, BS, heads_here, DH)
    far_keys = global_kv[..., :head_cols].reshape(NG, BS, heads_here, DH)
    far_values = global_kv[..., head_cols:].reshape(NG, BS, heads_here, DH)
    scores = (
        jnp.concatenate(
            [
                jnp.einsum(
                    "bqhd,bgkhd->bhqgk", query_heads, near_keys, preferred_element_type=jnp.float32
                ).reshape(blocks_here, heads_here, BS, near_count),
                jnp.einsum(
                    "bqhd,gkhd->bhqgk", query_heads, far_keys, preferred_element_type=jnp.float32
                ).reshape(blocks_here, heads_here, BS, NG * BS),
            ],
            axis=3,
        )
        * inv_root
    )
    block_ids = my_index * blocks_here + jnp.arange(blocks_here, dtype=jnp.int32)
    usable = jnp.concatenate(
        [
            (block_ids > 0)[:, None],
            jnp.ones((blocks_here, 1), bool),
            (block_ids < total_blocks - 1)[:, None],
            jnp.ones((blocks_here, NR + NG), bool),
        ],
        axis=1,
    )
    column_ok = jnp.repeat(usable, BS, axis=1)[:, None, None, :]
    masked = jnp.where(column_ok, scores, -jnp.inf)
    row_max = jnp.max(masked, axis=3, keepdims=True)
    log_total = row_max + jnp.log(jnp.sum(jnp.exp(masked - row_max), axis=3, keepdims=True))
    probs_full = jnp.exp(masked - log_total)
    probs_half = probs_full.astype(jnp.bfloat16)
    near_probs = probs_half[..., :near_count].reshape(blocks_here, heads_here, BS, near_groups, BS)
    far_probs = probs_half[..., near_count:].reshape(blocks_here, heads_here, BS, NG, BS)
    outputs = jnp.einsum(
        "bhqgk,bgkhd->bqhd", near_probs, near_values, preferred_element_type=jnp.float32
    ) + jnp.einsum("bhqgk,gkhd->bqhd", far_probs, far_values, preferred_element_type=jnp.float32)
    row_dot = jnp.sum(grad_heads.astype(jnp.float32) * outputs, axis=3)
    dprobs = jnp.concatenate(
        [
            jnp.einsum(
                "bqhd,bgkhd->bhqgk", grad_heads, near_values, preferred_element_type=jnp.float32
            ).reshape(blocks_here, heads_here, BS, near_count),
            jnp.einsum(
                "bqhd,gkhd->bhqgk", grad_heads, far_values, preferred_element_type=jnp.float32
            ).reshape(blocks_here, heads_here, BS, NG * BS),
        ],
        axis=3,
    )
    dscores = probs_full * (dprobs - jnp.transpose(row_dot, (0, 2, 1))[..., None])
    ds_half = dscores.astype(jnp.bfloat16)
    near_ds = ds_half[..., :near_count].reshape(blocks_here, heads_here, BS, near_groups, BS)
    far_ds = ds_half[..., near_count:].reshape(blocks_here, heads_here, BS, NG, BS)
    query_grad = (
        (
            (
                jnp.einsum(
                    "bhqgk,bgkhd->bqhd", near_ds, near_keys, preferred_element_type=jnp.float32
                )
                + jnp.einsum(
                    "bhqgk,gkhd->bqhd", far_ds, far_keys, preferred_element_type=jnp.float32
                )
            )
            * inv_root
        )
        .astype(jnp.bfloat16)
        .reshape(tokens, head_cols)
    )

    def key_value_parts(ds_part, probs_part):
        key_part = (
            jnp.einsum(
                "bhqgk,bqhd->bgkhd", ds_part, query_heads, preferred_element_type=jnp.float32
            )
            * inv_root
        )
        value_part = jnp.einsum(
            "bhqgk,bqhd->bgkhd", probs_part, grad_heads, preferred_element_type=jnp.float32
        )
        out_shape = key_part.shape[:3] + (head_cols,)
        return jnp.concatenate([key_part.reshape(out_shape), value_part.reshape(out_shape)], axis=3)

    random_part = key_value_parts(near_ds[:, :, :, 3:], near_probs[:, :, :, 3:])
    random_part = random_part.astype(jnp.bfloat16).reshape(entries, BS, 2 * head_cols)
    back_rows = (
        jnp.zeros((devices * capacity, BS, 2 * head_cols), jnp.bfloat16)
        .at[my_target]
        .set(random_part)
    )
    arrived = lax.all_to_all(back_rows, SEQ_AXES, split_axis=0, concat_axis=0, tiled=True)
    window_part = key_value_parts(near_ds[:, :, :, :3], near_probs[:, :, :, :3])
    zero_block = jnp.zeros((1, BS, 2 * head_cols), jnp.float32)
    own_grad = (
        window_part[:, 1]
        + jnp.concatenate([window_part[1:, 0], zero_block], axis=0)
        + jnp.concatenate([zero_block, window_part[:-1, 2]], axis=0)
    )
    rims_out = jnp.concatenate([window_part[0, 0], window_part[blocks_here - 1, 2]], axis=0)
    rims_in = with_halo(rims_out.astype(jnp.bfloat16), ALL_AXES, halo_up, BS).astype(rims_out.dtype)
    own_grad = own_grad.at[0].add(rims_in[:BS]).at[blocks_here - 1].add(rims_in[3 * BS :])
    far_key = (
        jnp.einsum("bhqgk,bqhd->gkhd", far_ds, query_heads, preferred_element_type=jnp.float32)
        * inv_root
    )
    far_value = jnp.einsum(
        "bhqgk,bqhd->gkhd", far_probs, grad_heads, preferred_element_type=jnp.float32
    )
    far_part = jnp.concatenate(
        [far_key.reshape(NG, BS, head_cols), far_value.reshape(NG, BS, head_cols)], axis=2
    )
    far_sum = all_sum(far_part, SEQ_AXES)
    here_ids = jnp.arange(blocks_here, dtype=jnp.int32)
    own_global = (
        (global_owner == my_index)[None, :] & (global_offset[None, :] == here_ids[:, None])
    ).astype(jnp.float32)
    own_grad = own_grad + jnp.einsum(
        "jg,gkc->jkc", own_global, far_sum, precision=lax.Precision.HIGHEST
    )
    weights = (served_used[None, :] & (served_block[None, :] == here_ids[:, None])).astype(
        jnp.bfloat16
    )
    own_grad = own_grad + jnp.einsum(
        "jr,rkc->jkc", weights, arrived, preferred_element_type=jnp.float32
    )
    key_grad = own_grad[..., :head_cols].astype(jnp.bfloat16).reshape(tokens, head_cols)
    value_grad = own_grad[..., head_cols:].astype(jnp.bfloat16).reshape(tokens, head_cols)
    outs = send_home(jnp.stack([query_grad, key_grad, value_grad]))
    return outs[0], outs[1], outs[2]


def solution(mesh):
    side = mesh.devices.shape[1] // 2
    grid = mesh.devices.reshape(-1, mesh.devices.shape[0] // (side * side), side, side, 2)
    cube = jax.sharding.Mesh(grid, ("zh", "zl", "y", "x", "core"))
    rows = ("zh", "zl", "y", "x", "core")
    placed = (P(rows, None),) * 4 + (P(), P())
    out = P(("zh", "zl", "y"), ("x", "core"))
    return jax.shard_map(
        per_device,
        mesh=cube,
        in_specs=placed,
        out_specs=(out, out, out),
        check_vma=False,
    )
```

```python
import math

import jax
import numpy as np
import jax.numpy as jnp
from jax import lax
from jax.sharding import PartitionSpec as P

DH = 128
BS = 32
NR = 3
NG = 4


def with_halo(x, axis, up, width):
    down = [(j, i) for i, j in up]
    length = x.shape[0]
    before = lax.ppermute(x[length - width :], axis, up)
    after = lax.ppermute(x[:width], axis, down)
    return jnp.concatenate([before, x, after], axis=0)


def chunk_sum(x, axis):
    peers = lax.axis_size(axis)
    parts = lax.all_to_all(x.reshape(peers, -1), axis, split_axis=0, concat_axis=0, tiled=True)
    return jnp.sum(parts.astype(jnp.float32), axis=0)


def chunk_share(chunk, axis, shape, dtype):
    peers = lax.axis_size(axis)
    copies = jnp.broadcast_to(chunk.astype(dtype)[None], (peers,) + chunk.shape)
    return lax.all_to_all(copies, axis, split_axis=0, concat_axis=0, tiled=True).reshape(shape)


def all_sum(x, axis):
    return chunk_share(chunk_sum(x, axis), axis, x.shape, x.dtype)


SEQ_AXES = ("zl", "y", "x")
SWAP_AXES = ("zh", "x")


ALL_AXES = ("zh", "zl", "y", "x", "core")


def move_slabs(x, forward):
    side = lax.axis_size("x")
    pairs = [(a * side + b, ((b - a) % side) * side + b) for a in range(side) for b in range(side)]
    if not forward:
        pairs = [(j, i) for i, j in pairs]
    return lax.ppermute(x, SWAP_AXES, pairs)


def shift_columns(x):
    side = lax.axis_size("x")
    pairs = [(a * side + b, a * side + (b - a) % side) for a in range(side) for b in range(side)]
    return lax.ppermute(x, SWAP_AXES, pairs)


def send_home(x):
    side = lax.axis_size("x")
    pairs = [(b * side + x, ((x - b) % side) * side + b) for b in range(side) for x in range(side)]
    return lax.ppermute(x, SWAP_AXES, pairs)


def layout_tables(sizes):
    hz, lz, ly, lx, cores = sizes
    ranges = lz * ly * lx
    slot = np.zeros((hz, ranges), np.int32)
    for b in range(hz):
        for r in range(ranges):
            slot[b, r] = ((r // ly) % lz) * (ly * lx) + (r % ly) * lx + (r // (lz * ly) + b) % lx
    up = []
    for b in range(hz):
        for c in range(cores):
            for r in range(ranges - 1):
                here, there = slot[b, r], slot[b, r + 1]
                up.append(((b * ranges + here) * cores + c, (b * ranges + there) * cores + c))
    return slot, np.argsort(slot, axis=1).astype(np.int32), up


def per_device(queries, key_states, value_states, out_grad, random_blocks, global_blocks):
    groups = lax.axis_size(("x", "core"))
    rows_in, cols_in = queries.shape
    stacked = jnp.stack([queries, key_states, value_states, out_grad], axis=1)
    sizes = tuple(lax.axis_size(a) for a in ALL_AXES)
    stacked = stacked.reshape(rows_in, 4, sizes[3], groups // sizes[3], cols_in // groups)
    stacked = jnp.roll(stacked, lax.axis_index("zh"), axis=2)
    stacked = stacked.reshape(rows_in, 4, groups, cols_in // groups)
    stacked = lax.all_to_all(stacked, ("x", "core"), split_axis=2, concat_axis=0, tiled=True)
    stacked = move_slabs(stacked, True)
    query_rows, key_rows, value_rows, grad_rows = (stacked[:, i, 0] for i in range(4))
    tokens = query_rows.shape[0]
    head_cols = query_rows.shape[1]
    heads_here = head_cols // DH
    blocks_here = tokens // BS
    lz, ly, lx = (lax.axis_size(a) for a in SEQ_AXES)
    devices = lz * ly * lx
    slab = lax.axis_index("zh")
    my_index = ((lax.axis_index("x") - slab) % lx * lz + lax.axis_index("zl")) * ly + lax.axis_index("y")
    slot_table, range_table, halo_up = layout_tables(sizes)
    slot_of = jnp.asarray(slot_table)[slab]
    range_at = jnp.asarray(range_table)[slab]
    total_blocks = devices * blocks_here
    entries = blocks_here * NR
    capacity = (entries + devices - 1) // devices
    inv_root = 1.0 / math.sqrt(DH)
    kv_rows = jnp.concatenate([key_rows, value_rows], axis=1)
    kv_blocks = kv_rows.reshape(blocks_here, BS, 2 * head_cols)
    extended = with_halo(kv_rows, ALL_AXES, halo_up, BS)
    extended = extended.reshape(blocks_here + 2, BS, 2 * head_cols)
    window = jnp.stack(
        [extended[:blocks_here], extended[1 : blocks_here + 1], extended[2:]], axis=1
    )
    global_owner = global_blocks // blocks_here
    global_offset = global_blocks % blocks_here
    owned = jnp.take(kv_blocks, global_offset, axis=0)
    owned = jnp.where((global_owner == my_index)[:, None, None], owned, jnp.zeros_like(owned))
    global_kv = all_sum(owned, SEQ_AXES)
    entry_table = random_blocks.reshape(devices, entries)
    table_owner = entry_table // blocks_here
    table_offset = entry_table % blocks_here
    positions = jnp.arange(entries, dtype=jnp.int32)
    before = positions[None, :] < positions[:, None]
    matches = (table_owner[:, :, None] == table_owner[:, None, :]) & before[None]
    table_slot = jnp.sum(matches.astype(jnp.int32), axis=2)
    my_owner = lax.dynamic_index_in_dim(table_owner, my_index, 0, keepdims=False)
    my_slot = lax.dynamic_index_in_dim(table_slot, my_index, 0, keepdims=False)
    my_target = slot_of[my_owner] * capacity + my_slot
    slot_ids = jnp.arange(capacity, dtype=jnp.int32)
    served = (table_owner == my_index)[:, :, None] & (
        table_slot[:, :, None] == slot_ids[None, None, :]
    )
    served_block = jnp.sum(jnp.where(served, table_offset[:, :, None], 0), axis=1)[range_at].reshape(-1)
    served_used = jnp.any(served, axis=1)[range_at].reshape(-1)
    outgoing = jnp.take(kv_blocks, served_block, axis=0)
    incoming = lax.all_to_all(outgoing, SEQ_AXES, split_axis=0, concat_axis=0, tiled=True)
    fetched = jnp.take(incoming, my_target, axis=0).reshape(blocks_here, NR, BS, 2 * head_cols)
    near_kv = jnp.concatenate([window, fetched], axis=1)
    near_groups = 3 + NR
    near_count = near_groups * BS
    query_heads = query_rows.reshape(blocks_here, BS, heads_here, DH)
    grad_heads = grad_rows.reshape(blocks_here, BS, heads_here, DH)
    near_keys = near_kv[..., :head_cols].reshape(blocks_here, near_groups, BS, heads_here, DH)
    near_values = near_kv[..., head_cols:].reshape(blocks_here, near_groups, BS, heads_here, DH)
    far_keys = global_kv[..., :head_cols].reshape(NG, BS, heads_here, DH)
    far_values = global_kv[..., head_cols:].reshape(NG, BS, heads_here, DH)
    scores = (
        jnp.concatenate(
            [
                jnp.einsum(
                    "bqhd,bgkhd->bhqgk", query_heads, near_keys, preferred_element_type=jnp.float32
                ).reshape(blocks_here, heads_here, BS, near_count),
                jnp.einsum(
                    "bqhd,gkhd->bhqgk", query_heads, far_keys, preferred_element_type=jnp.float32
                ).reshape(blocks_here, heads_here, BS, NG * BS),
            ],
            axis=3,
        )
        * inv_root
    )
    block_ids = my_index * blocks_here + jnp.arange(blocks_here, dtype=jnp.int32)
    usable = jnp.concatenate(
        [
            (block_ids > 0)[:, None],
            jnp.ones((blocks_here, 1), bool),
            (block_ids < total_blocks - 1)[:, None],
            jnp.ones((blocks_here, NR + NG), bool),
        ],
        axis=1,
    )
    column_ok = jnp.repeat(usable, BS, axis=1)[:, None, None, :]
    masked = jnp.where(column_ok, scores, -jnp.inf)
    row_max = jnp.max(masked, axis=3, keepdims=True)
    log_total = row_max + jnp.log(jnp.sum(jnp.exp(masked - row_max), axis=3, keepdims=True))
    probs_full = jnp.exp(masked - log_total)
    probs_half = probs_full.astype(jnp.bfloat16)
    near_probs = probs_half[..., :near_count].reshape(blocks_here, heads_here, BS, near_groups, BS)
    far_probs = probs_half[..., near_count:].reshape(blocks_here, heads_here, BS, NG, BS)
    outputs = jnp.einsum(
        "bhqgk,bgkhd->bqhd", near_probs, near_values, preferred_element_type=jnp.float32
    ) + jnp.einsum("bhqgk,gkhd->bqhd", far_probs, far_values, preferred_element_type=jnp.float32)
    row_dot = jnp.sum(grad_heads.astype(jnp.float32) * outputs, axis=3)
    dprobs = jnp.concatenate(
        [
            jnp.einsum(
                "bqhd,bgkhd->bhqgk", grad_heads, near_values, preferred_element_type=jnp.float32
            ).reshape(blocks_here, heads_here, BS, near_count),
            jnp.einsum(
                "bqhd,gkhd->bhqgk", grad_heads, far_values, preferred_element_type=jnp.float32
            ).reshape(blocks_here, heads_here, BS, NG * BS),
        ],
        axis=3,
    )
    dscores = probs_full * (dprobs - jnp.transpose(row_dot, (0, 2, 1))[..., None])
    ds_half = dscores.astype(jnp.bfloat16)
    near_ds = ds_half[..., :near_count].reshape(blocks_here, heads_here, BS, near_groups, BS)
    far_ds = ds_half[..., near_count:].reshape(blocks_here, heads_here, BS, NG, BS)
    query_grad = (
        (
            (
                jnp.einsum(
                    "bhqgk,bgkhd->bqhd", near_ds, near_keys, preferred_element_type=jnp.float32
                )
                + jnp.einsum(
                    "bhqgk,gkhd->bqhd", far_ds, far_keys, preferred_element_type=jnp.float32
                )
            )
            * inv_root
        )
        .astype(jnp.bfloat16)
        .reshape(tokens, head_cols)
    )

    def key_value_parts(ds_part, probs_part):
        key_part = (
            jnp.einsum(
                "bhqgk,bqhd->bgkhd", ds_part, query_heads, preferred_element_type=jnp.float32
            )
            * inv_root
        )
        value_part = jnp.einsum(
            "bhqgk,bqhd->bgkhd", probs_part, grad_heads, preferred_element_type=jnp.float32
        )
        out_shape = key_part.shape[:3] + (head_cols,)
        return jnp.concatenate([key_part.reshape(out_shape), value_part.reshape(out_shape)], axis=3)

    random_part = key_value_parts(near_ds[:, :, :, 3:], near_probs[:, :, :, 3:])
    random_part = random_part.astype(jnp.bfloat16).reshape(entries, BS, 2 * head_cols)
    back_rows = (
        jnp.zeros((devices * capacity, BS, 2 * head_cols), jnp.bfloat16)
        .at[my_target]
        .set(random_part)
    )
    arrived = lax.all_to_all(back_rows, SEQ_AXES, split_axis=0, concat_axis=0, tiled=True)
    window_part = key_value_parts(near_ds[:, :, :, :3], near_probs[:, :, :, :3])
    zero_block = jnp.zeros((1, BS, 2 * head_cols), jnp.float32)
    own_grad = (
        window_part[:, 1]
        + jnp.concatenate([window_part[1:, 0], zero_block], axis=0)
        + jnp.concatenate([zero_block, window_part[:-1, 2]], axis=0)
    )
    rims_out = jnp.concatenate([window_part[0, 0], window_part[blocks_here - 1, 2]], axis=0)
    rims_in = with_halo(rims_out.astype(jnp.bfloat16), ALL_AXES, halo_up, BS).astype(rims_out.dtype)
    own_grad = own_grad.at[0].add(rims_in[:BS]).at[blocks_here - 1].add(rims_in[3 * BS :])
    far_key = (
        jnp.einsum("bhqgk,bqhd->gkhd", far_ds, query_heads, preferred_element_type=jnp.float32)
        * inv_root
    )
    far_value = jnp.einsum(
        "bhqgk,bqhd->gkhd", far_probs, grad_heads, preferred_element_type=jnp.float32
    )
    far_part = jnp.concatenate(
        [far_key.reshape(NG, BS, head_cols), far_value.reshape(NG, BS, head_cols)], axis=2
    )
    far_sum = all_sum(far_part, SEQ_AXES)
    here_ids = jnp.arange(blocks_here, dtype=jnp.int32)
    own_global = (
        (global_owner == my_index)[None, :] & (global_offset[None, :] == here_ids[:, None])
    ).astype(jnp.float32)
    own_grad = own_grad + jnp.einsum(
        "jg,gkc->jkc", own_global, far_sum, precision=lax.Precision.HIGHEST
    )
    weights = (served_used[None, :] & (served_block[None, :] == here_ids[:, None])).astype(
        jnp.bfloat16
    )
    own_grad = own_grad + jnp.dot(
        weights, arrived.reshape(arrived.shape[0], -1), preferred_element_type=jnp.float32
    ).reshape(own_grad.shape)
    key_grad = own_grad[..., :head_cols].astype(jnp.bfloat16).reshape(tokens, head_cols)
    value_grad = own_grad[..., head_cols:].astype(jnp.bfloat16).reshape(tokens, head_cols)
    outs = send_home(jnp.stack([query_grad, key_grad, value_grad]))
    return outs[0], outs[1], outs[2]


def solution(mesh):
    side = mesh.devices.shape[1] // 2
    grid = mesh.devices.reshape(-1, mesh.devices.shape[0] // (side * side), side, side, 2)
    cube = jax.sharding.Mesh(grid, ("zh", "zl", "y", "x", "core"))
    rows = ("zh", "zl", "y", "x", "core")
    placed = (P(rows, None),) * 4 + (P(), P())
    out = P(("zh", "zl", "y"), ("x", "core"))
    return jax.shard_map(
        per_device,
        mesh=cube,
        in_specs=placed,
        out_specs=(out, out, out),
        check_vma=False,
    )
```
